32 devices in a mesh: row: 4 (over y, x), col: 8 (over z, core).
Axes of the slice: x: 2, y: 2, z: 4, core: 2. Of those that a mesh axis runs over, the one named last changes fastest.
Arguments:
- tokens: bfloat16 [256, 12288], P('col', 'row'), may hold values from -6 to 6
- weight: bfloat16 [12288, 24576], P('row', 'col'), may hold values from -0.0546875 to 0.0546875
- bias: float32 [24576], P('col'), may hold values from -4 to 4
- cotangent: bfloat16 [256, 24576], P(None, 'col'), may hold values from -6 to 6
Outputs:
- hidden: bfloat16 [256, 24576], P('row', 'col')
- grad_tokens: bfloat16 [256, 12288], P('col', 'row')
- grad_weight: bfloat16 [12288, 24576], P('row', 'col')
- grad_bias: float32 [24576], P('col')
The draws below stay inside these ranges and needn't reach their ends.
All inputs are finite; a program needn't handle non-finite values.
Results may differ from the reference program's by a relative error of at most 0.0055.
Values may be sent and summed in bfloat16 or wider, within the bound.
No kernel may reach another device: no remote copies, remote signals or barrier semaphores. Data moves between devices by JAX's collectives and lax.ppermute only.
A program may use at most 192 MiB of HBM per device.

```python
import math
import jax
import jax.numpy as jnp
from jax import lax

D = 12288
FF = 24576
TOKENS = 256


def block_scale(stream_key, shape, shards, least, top_value):
    loudness = 1.0
    for axis_at, shards_of in shards:
        draws = jax.random.uniform(jax.random.fold_in(jax.random.fold_in(stream_key, 6), axis_at), (shards_of,), jnp.float32, least / len(shards), top_value / len(shards))
        loudness = loudness * jnp.repeat(jnp.exp(draws), shape[axis_at] // shards_of).reshape((-1,) + (1,) * (len(shape) - 1 - axis_at))
    return loudness


def bell_draw(own_key, shape, width, reach, cuts=(), kind=jnp.bfloat16):
    drawn = width * jax.random.normal(own_key, shape, jnp.float32)
    if cuts:
        drawn = drawn * block_scale(own_key, shape, cuts, -0.22, 0.18)
    return jnp.clip(drawn, -reach, reach).astype(kind)


def setup_inputs(seed: int = 0) -> dict:
    streams_of = jax.random.split(jax.random.key(seed), 5)
    tokens = bell_draw(streams_of[0], (TOKENS, D), 1.0, 6.0, ((0, 8), (1, 4)))
    weight = bell_draw(streams_of[1], (D, FF), D ** -0.5, 0.0546875, ((0, 4), (1, 8)))
    bias = bell_draw(streams_of[2], (FF,), 1.0, 4.0, ((0, 8),), jnp.float32)
    cotangent = bell_draw(streams_of[3], (TOKENS, FF), 1.0, 6.0, ((1, 8),))
    return dict(tokens=tokens, weight=weight, bias=bias, cotangent=cotangent)


def reference(tokens, weight, bias, cotangent):
    preact = jnp.dot(tokens, weight, preferred_element_type=jnp.float32) + bias.astype(jnp.float32)
    normal_cdf = 0.5 * (1.0 + jax.scipy.special.erf(preact / math.sqrt(2.0)))
    normal_pdf = jnp.exp(-0.5 * preact * preact) / math.sqrt(2.0 * math.pi)
    hidden = (preact * normal_cdf).astype(jnp.bfloat16)
    grad_pre = (cotangent.astype(jnp.float32) * (normal_cdf + preact * normal_pdf)).astype(jnp.bfloat16)
    grad_tokens = jnp.dot(grad_pre, weight.T, preferred_element_type=jnp.float32).astype(jnp.bfloat16)
    grad_weight = jnp.dot(tokens.T, grad_pre, preferred_element_type=jnp.float32).astype(jnp.bfloat16)
    grad_bias = lax.optimization_barrier(jnp.sum(grad_pre.astype(jnp.float32), axis=0))
    return (hidden, grad_tokens, grad_weight, grad_bias)
```

```python
import math

import jax
import jax.numpy as jnp
from jax import lax
from jax.experimental import pallas as pl
from jax.experimental.pallas import tpu as pltpu
from jax.sharding import PartitionSpec as P


def activate(preact, cotangent):
    normal_cdf = 0.5 * (1.0 + jax.scipy.special.erf(preact / math.sqrt(2.0)))
    normal_pdf = jnp.exp(-0.5 * preact * preact) / math.sqrt(2.0 * math.pi)
    hidden = (preact * normal_cdf).astype(jnp.bfloat16)
    grad_pre = (cotangent.astype(jnp.float32) * (normal_cdf + preact * normal_pdf)).astype(
        jnp.bfloat16
    )
    return (hidden, grad_pre)


def _outer_kernel(xt_ref, g_ref, o_ref):
    o_ref[...] = jnp.dot(xt_ref[...], g_ref[...], preferred_element_type=jnp.float32).astype(
        o_ref.dtype
    )


def outer_product_sum(xt, g, block_m=512, block_n=1536):
    m, k = xt.shape
    n = g.shape[1]
    block_m = min(block_m, m)
    block_n = min(block_n, n)
    return pl.pallas_call(
        _outer_kernel,
        grid=(n // block_n, m // block_m),
        in_specs=[
            pl.BlockSpec((block_m, k), lambda j, i: (i, 0)),
            pl.BlockSpec((k, block_n), lambda j, i: (0, j)),
        ],
        out_specs=pl.BlockSpec((block_m, block_n), lambda j, i: (i, j)),
        out_shape=jax.ShapeDtypeStruct((m, n), jnp.bfloat16),
        cost_estimate=pl.CostEstimate(
            flops=2 * m * n * k, transcendentals=0, bytes_accessed=2 * (m * k + k * n + m * n)
        ),
    )(xt, g)


def body(tokens, weight, bias, cotangent):
    local_x = lax.all_gather(tokens, "col", axis=0, tiled=True)
    my_rows = local_x.shape[0] // lax.axis_size("row")
    first_row = lax.axis_index("row") * my_rows
    partial_value = jnp.dot(local_x, weight, preferred_element_type=jnp.float32)
    preact = lax.psum_scatter(partial_value, "row", scatter_dimension=0, tiled=True) + bias
    my_cot = lax.dynamic_slice_in_dim(cotangent, first_row, my_rows, 0)
    hidden, my_grad = activate(preact, my_cot)
    full_grad = lax.all_gather(my_grad, "row", axis=0, tiled=True)
    grad_tokens = lax.psum_scatter(
        lax.dot_general(
            full_grad, weight, (((1,), (1,)), ((), ())), preferred_element_type=jnp.float32
        ),
        "col",
        scatter_dimension=0,
        tiled=True,
    ).astype(jnp.bfloat16)
    grad_weight = outer_product_sum(local_x.T, full_grad)
    grad_bias = jnp.sum(full_grad.astype(jnp.float32), axis=0)
    return (hidden, grad_tokens, grad_weight, grad_bias)


def solution(mesh):
    placed = (P("col", "row"), P("row", "col"), P("col"), P(None, "col"))
    return jax.shard_map(
        body,
        mesh=mesh,
        in_specs=placed,
        out_specs=(P("row", "col"), P("col", "row"), P("row", "col"), P("col")),
        check_vma=False,
    )
```

```python
import math

import jax
import jax.numpy as jnp
from jax import lax
from jax.experimental import pallas as pl
from jax.experimental.pallas import tpu as pltpu
from jax.sharding import PartitionSpec as P


def activate(preact, cotangent):
    normal_cdf = 0.5 * (1.0 + jax.scipy.special.erf(preact / math.sqrt(2.0)))
    normal_pdf = jnp.exp(-0.5 * preact * preact) / math.sqrt(2.0 * math.pi)
    hidden = (preact * normal_cdf).astype(jnp.bfloat16)
    grad_pre = (cotangent.astype(jnp.float32) * (normal_cdf + preact * normal_pdf)).astype(
        jnp.bfloat16
    )
    return (hidden, grad_pre)


def _outer_kernel(xt_ref, g_ref, o_ref):
    o_ref[...] = jnp.dot(xt_ref[...], g_ref[...], preferred_element_type=jnp.float32).astype(
        o_ref.dtype
    )


def outer_product_sum(xt, g, block_m=512, block_n=1536):
    m, k = xt.shape
    n = g.shape[1]
    block_m = min(block_m, m)
    block_n = min(block_n, n)
    return pl.pallas_call(
        _outer_kernel,
        grid=(n // block_n, m // block_m),
        in_specs=[
            pl.BlockSpec((block_m, k), lambda j, i: (i, 0)),
            pl.BlockSpec((k, block_n), lambda j, i: (0, j)),
        ],
        out_specs=pl.BlockSpec((block_m, block_n), lambda j, i: (i, j)),
        out_shape=jax.ShapeDtypeStruct((m, n), jnp.bfloat16),
        cost_estimate=pl.CostEstimate(
            flops=2 * m * n * k, transcendentals=0, bytes_accessed=2 * (m * k + k * n + m * n)
        ),
    )(xt, g)


def _swap(value, axis, flip):
    size = lax.axis_size(axis)
    return lax.ppermute(value, axis, [(i, i ^ flip) for i in range(size)])


def _pick(index, blocks):
    return lax.dynamic_index_in_dim(blocks, index, axis=0, keepdims=False)


def _halves(value):
    cols = value.shape[1]
    if cols % 256:
        return [value]
    return [value[:, : cols // 2], value[:, cols // 2 :]]


def _bit_orders(n):
    order = list(range(n.bit_length() - 1))
    return [order, order[::-1]]


def row_reduce_scatter(partial, axis="row"):
    n = lax.axis_size(axis)
    if n & (n - 1):
        return lax.psum_scatter(partial, axis, scatter_dimension=0, tiled=True)
    levels = n.bit_length() - 1
    r = lax.axis_index(axis)
    m = partial.shape[0] // n
    outs = []
    for half, order in zip(_halves(partial), _bit_orders(n)):
        cur = half.reshape([2] * levels + [m, half.shape[1]])
        bits = list(range(levels))[::-1]
        for bit in order:
            mine = (r >> bit) & 1
            t = jnp.moveaxis(cur, bits.index(bit), 0)
            sent = _swap(_pick(1 - mine, t).astype(jnp.bfloat16), axis, 1 << bit)
            cur = _pick(mine, t) + sent.astype(jnp.float32)
            bits.remove(bit)
        outs.append(cur.reshape(m, half.shape[1]))
    return jnp.concatenate(outs, axis=1)


def _pair(mine, theirs, bit):
    first = jnp.where(bit == 0, mine, theirs)
    second = jnp.where(bit == 0, theirs, mine)
    return jnp.stack([first, second], axis=0)


def row_all_gather(block, axis="row"):
    n = lax.axis_size(axis)
    if n & (n - 1):
        return lax.all_gather(block, axis, axis=0, tiled=True)
    levels = n.bit_length() - 1
    r = lax.axis_index(axis)
    m = block.shape[0]
    outs = []
    for half, order in zip(_halves(block), _bit_orders(n)):
        cur = half
        bits = []
        for bit in order:
            cur = _pair(cur, _swap(cur, axis, 1 << bit), (r >> bit) & 1)
            bits.insert(0, bit)
        perm = sorted(range(levels), key=lambda j: -bits[j])
        cur = jnp.transpose(cur, perm + [levels, levels + 1])
        outs.append(cur.reshape(n * m, half.shape[1]))
    return jnp.concatenate(outs, axis=1)


def body(tokens, weight, bias, cotangent):
    local_x = lax.all_gather(tokens, "col", axis=0, tiled=True)
    my_rows = local_x.shape[0] // lax.axis_size("row")
    first_row = lax.axis_index("row") * my_rows
    partial_value = jnp.dot(local_x, weight, preferred_element_type=jnp.float32)
    preact = row_reduce_scatter(partial_value) + bias
    my_cot = lax.dynamic_slice_in_dim(cotangent, first_row, my_rows, 0)
    hidden, my_grad = activate(preact, my_cot)
    full_grad = row_all_gather(my_grad)
    grad_tokens = lax.psum_scatter(
        lax.dot_general(
            full_grad, weight, (((1,), (1,)), ((), ())), preferred_element_type=jnp.float32
        ),
        "col",
        scatter_dimension=0,
        tiled=True,
    ).astype(jnp.bfloat16)
    grad_weight = outer_product_sum(local_x.T, full_grad)
    grad_bias = jnp.sum(full_grad.astype(jnp.float32), axis=0)
    return (hidden, grad_tokens, grad_weight, grad_bias)


def solution(mesh):
    placed = (P("col", "row"), P("row", "col"), P("col"), P(None, "col"))
    return jax.shard_map(
        body,
        mesh=mesh,
        in_specs=placed,
        out_specs=(P("row", "col"), P("col", "row"), P("row", "col"), P("col")),
        check_vma=False,
    )
```

```python
import math

import jax
import jax.numpy as jnp
from jax import lax
from jax.experimental import pallas as pl
from jax.experimental.pallas import tpu as pltpu
from jax.sharding import PartitionSpec as P


def activate(preact, cotangent):
    normal_cdf = 0.5 * (1.0 + jax.scipy.special.erf(preact / math.sqrt(2.0)))
    normal_pdf = jnp.exp(-0.5 * preact * preact) / math.sqrt(2.0 * math.pi)
    hidden = (preact * normal_cdf).astype(jnp.bfloat16)
    grad_pre = (cotangent.astype(jnp.float32) * (normal_cdf + preact * normal_pdf)).astype(
        jnp.bfloat16
    )
    return (hidden, grad_pre)


def _outer_kernel(xt_ref, g_ref, o_ref):
    o_ref[...] = jnp.dot(xt_ref[...], g_ref[...], preferred_element_type=jnp.float32).astype(
        o_ref.dtype
    )


def outer_product_sum(xt, g, block_m=512, block_n=1536):
    m, k = xt.shape
    n = g.shape[1]
    block_m = min(block_m, m)
    block_n = min(block_n, n)
    return pl.pallas_call(
        _outer_kernel,
        grid=(n // block_n, m // block_m),
        in_specs=[
            pl.BlockSpec((block_m, k), lambda j, i: (i, 0)),
            pl.BlockSpec((k, block_n), lambda j, i: (0, j)),
        ],
        out_specs=pl.BlockSpec((block_m, block_n), lambda j, i: (i, j)),
        out_shape=jax.ShapeDtypeStruct((m, n), jnp.bfloat16),
        cost_estimate=pl.CostEstimate(
            flops=2 * m * n * k, transcendentals=0, bytes_accessed=2 * (m * k + k * n + m * n)
        ),
    )(xt, g)


def _swap(value, axis, flip):
    size = lax.axis_size(axis)
    return lax.ppermute(value, axis, [(i, i ^ flip) for i in range(size)])


def _pick(index, blocks):
    return lax.dynamic_index_in_dim(blocks, index, axis=0, keepdims=False)


def _halves(value):
    cols = value.shape[1]
    if cols % 256:
        return [value]
    return [value[:, : cols // 2], value[:, cols // 2 :]]


def _bit_orders(n):
    order = list(range(n.bit_length() - 1))
    return [order, order[::-1]]


def row_reduce_scatter(partial, axis="row"):
    n = lax.axis_size(axis)
    if n & (n - 1):
        return lax.psum_scatter(partial, axis, scatter_dimension=0, tiled=True)
    levels = n.bit_length() - 1
    r = lax.axis_index(axis)
    m = partial.shape[0] // n
    outs = []
    for half, order in zip(_halves(partial), _bit_orders(n)):
        cur = half.reshape([2] * levels + [m, half.shape[1]])
        bits = list(range(levels))[::-1]
        for bit in order:
            mine = (r >> bit) & 1
            t = jnp.moveaxis(cur, bits.index(bit), 0)
            sent = _swap(_pick(1 - mine, t).astype(jnp.bfloat16), axis, 1 << bit)
            cur = _pick(mine, t) + sent.astype(jnp.float32)
            bits.remove(bit)
        outs.append(cur.reshape(m, half.shape[1]))
    return jnp.concatenate(outs, axis=1)


def _pair(mine, theirs, bit):
    first = jnp.where(bit == 0, mine, theirs)
    second = jnp.where(bit == 0, theirs, mine)
    return jnp.stack([first, second], axis=0)


def row_all_gather(block, axis="row"):
    n = lax.axis_size(axis)
    if n & (n - 1):
        return lax.all_gather(block, axis, axis=0, tiled=True)
    levels = n.bit_length() - 1
    r = lax.axis_index(axis)
    m = block.shape[0]
    outs = []
    for half, order in zip(_halves(block), _bit_orders(n)):
        cur = half
        bits = []
        for bit in order:
            cur = _pair(cur, _swap(cur, axis, 1 << bit), (r >> bit) & 1)
            bits.insert(0, bit)
        perm = sorted(range(levels), key=lambda j: -bits[j])
        cur = jnp.transpose(cur, perm + [levels, levels + 1])
        outs.append(cur.reshape(n * m, half.shape[1]))
    return jnp.concatenate(outs, axis=1)


def _chain_pairs(chips, step):
    return [
        (2 * z + k, 2 * (z + step) + k)
        for z in range(chips)
        if 0 <= z + step < chips
        for k in range(2)
    ]


def col_all_gather(block, axis="col"):
    n = lax.axis_size(axis)
    if n % 2:
        return lax.all_gather(block, axis, axis=0, tiled=True)
    chips = n // 2
    c = lax.axis_index(axis)
    z, k = c // 2, c % 2
    from_left, from_right = [], []
    going_right = going_left = block
    for _ in range(chips - 1):
        going_right = lax.ppermute(going_right, axis, _chain_pairs(chips, 1))
        going_left = lax.ppermute(going_left, axis, _chain_pairs(chips, -1))
        from_left.append(going_right)
        from_right.append(going_left)
    held = jnp.stack([block] + from_left + from_right)
    mine = []
    for j in range(chips):
        at = jnp.where(j == z, 0, jnp.where(j < z, z - j, chips - 1 + j - z))
        mine.append(_pick(at, held))
    mine = jnp.stack(mine)
    both = _pair(mine, _swap(mine, axis, 1), k)
    return jnp.swapaxes(both, 0, 1).reshape(n * block.shape[0], block.shape[1])


def col_reduce_scatter(partial, axis="col"):
    n = lax.axis_size(axis)
    if n % 2:
        return lax.psum_scatter(partial, axis, scatter_dimension=0, tiled=True)
    chips = n // 2
    m = partial.shape[0] // n
    c = lax.axis_index(axis)
    z, k = c // 2, c % 2
    by_core = jnp.swapaxes(partial.reshape(chips, 2, m, partial.shape[1]), 0, 1)
    chip = _pick(k, by_core) + _swap(_pick(1 - k, by_core), axis, 1)
    to_right = to_left = jnp.zeros_like(chip[0])
    for step in range(1, chips):
        to_right = lax.ppermute(
            _pick(z + chips - step, chip) + to_right, axis, _chain_pairs(chips, 1)
        )
        to_left = lax.ppermute(
            _pick(z - chips + step, chip) + to_left, axis, _chain_pairs(chips, -1)
        )
    return _pick(z, chip) + to_right + to_left


def body(tokens, weight, bias, cotangent):
    local_x = col_all_gather(tokens)
    my_rows = local_x.shape[0] // lax.axis_size("row")
    first_row = lax.axis_index("row") * my_rows
    partial_value = jnp.dot(local_x, weight, preferred_element_type=jnp.float32)
    preact = row_reduce_scatter(partial_value) + bias
    my_cot = lax.dynamic_slice_in_dim(cotangent, first_row, my_rows, 0)
    hidden, my_grad = activate(preact, my_cot)
    full_grad = row_all_gather(my_grad)
    grad_tokens = col_reduce_scatter(
        lax.dot_general(
            full_grad, weight, (((1,), (1,)), ((), ())), preferred_element_type=jnp.float32
        )
    ).astype(jnp.bfloat16)
    grad_weight = outer_product_sum(local_x.T, full_grad)
    grad_bias = jnp.sum(full_grad.astype(jnp.float32), axis=0)
    return (hidden, grad_tokens, grad_weight, grad_bias)


def solution(mesh):
    placed = (P("col", "row"), P("row", "col"), P("col"), P(None, "col"))
    return jax.shard_map(
        body,
        mesh=mesh,
        in_specs=placed,
        out_specs=(P("row", "col"), P("col", "row"), P("row", "col"), P("col")),
        check_vma=False,
    )
```

```python
import math

import jax
import jax.numpy as jnp
from jax import lax
from jax.experimental import pallas as pl
from jax.experimental.pallas import tpu as pltpu
from jax.sharding import PartitionSpec as P


def activate(preact, cotangent):
    normal_cdf = 0.5 * (1.0 + jax.scipy.special.erf(preact / math.sqrt(2.0)))
    normal_pdf = jnp.exp(-0.5 * preact * preact) / math.sqrt(2.0 * math.pi)
    hidden = (preact * normal_cdf).astype(jnp.bfloat16)
    grad_pre = (cotangent.astype(jnp.float32) * (normal_cdf + preact * normal_pdf)).astype(
        jnp.bfloat16
    )
    return (hidden, grad_pre)


def _outer_kernel(xt_ref, g_ref, o_ref):
    o_ref[...] = jnp.dot(xt_ref[...], g_ref[...], preferred_element_type=jnp.float32).astype(
        o_ref.dtype
    )


def outer_product_sum(xt, g, block_m=512, block_n=1536):
    m, k = xt.shape
    n = g.shape[1]
    block_m = min(block_m, m)
    block_n = min(block_n, n)
    return pl.pallas_call(
        _outer_kernel,
        grid=(n // block_n, m // block_m),
        in_specs=[
            pl.BlockSpec((block_m, k), lambda j, i: (i, 0)),
            pl.BlockSpec((k, block_n), lambda j, i: (0, j)),
        ],
        out_specs=pl.BlockSpec((block_m, block_n), lambda j, i: (i, j)),
        out_shape=jax.ShapeDtypeStruct((m, n), jnp.bfloat16),
        cost_estimate=pl.CostEstimate(
            flops=2 * m * n * k, transcendentals=0, bytes_accessed=2 * (m * k + k * n + m * n)
        ),
    )(xt, g)


def _swap(value, axis, flip):
    size = lax.axis_size(axis)
    return lax.ppermute(value, axis, [(i, i ^ flip) for i in range(size)])


def _pick(index, blocks):
    return lax.dynamic_index_in_dim(blocks, index, axis=0, keepdims=False)


def _halves(value):
    cols = value.shape[1]
    if cols % 256:
        return [value]
    return [value[:, : cols // 2], value[:, cols // 2 :]]


def _bit_orders(n):
    order = list(range(n.bit_length() - 1))
    return [order, order[::-1]]


def row_reduce_scatter(partial, axis="row"):
    n = lax.axis_size(axis)
    if n & (n - 1):
        return lax.psum_scatter(partial, axis, scatter_dimension=0, tiled=True)
    levels = n.bit_length() - 1
    r = lax.axis_index(axis)
    m = partial.shape[0] // n
    outs = []
    for half, order in zip(_halves(partial), _bit_orders(n)):
        cur = half.reshape([2] * levels + [m, half.shape[1]])
        bits = list(range(levels))[::-1]
        for bit in order:
            mine = (r >> bit) & 1
            t = jnp.moveaxis(cur, bits.index(bit), 0)
            sent = _swap(_pick(1 - mine, t).astype(jnp.bfloat16), axis, 1 << bit)
            cur = _pick(mine, t) + sent.astype(jnp.float32)
            bits.remove(bit)
        outs.append(cur.reshape(m, half.shape[1]))
    return jnp.concatenate(outs, axis=1)


def _pair(mine, theirs, bit):
    first = jnp.where(bit == 0, mine, theirs)
    second = jnp.where(bit == 0, theirs, mine)
    return jnp.stack([first, second], axis=0)


def row_all_gather(block, axis="row"):
    n = lax.axis_size(axis)
    if n & (n - 1):
        return lax.all_gather(block, axis, axis=0, tiled=True)
    levels = n.bit_length() - 1
    r = lax.axis_index(axis)
    m = block.shape[0]
    outs = []
    for half, order in zip(_halves(block), _bit_orders(n)):
        cur = half
        bits = []
        for bit in order:
            cur = _pair(cur, _swap(cur, axis, 1 << bit), (r >> bit) & 1)
            bits.insert(0, bit)
        perm = sorted(range(levels), key=lambda j: -bits[j])
        cur = jnp.transpose(cur, perm + [levels, levels + 1])
        outs.append(cur.reshape(n * m, half.shape[1]))
    return jnp.concatenate(outs, axis=1)


def col_all_gather(block, axis="col"):
    n = lax.axis_size(axis)
    if n % 2:
        return lax.all_gather(block, axis, axis=0, tiled=True)
    groups = [list(range(k, n, 2)) for k in range(2)]
    mine = lax.all_gather(block, axis, axis_index_groups=groups)
    both = _pair(mine, _swap(mine, axis, 1), lax.axis_index(axis) % 2)
    return jnp.swapaxes(both, 0, 1).reshape(n * block.shape[0], block.shape[1])


def body(tokens, weight, bias, cotangent):
    local_x = col_all_gather(tokens)
    my_rows = local_x.shape[0] // lax.axis_size("row")
    first_row = lax.axis_index("row") * my_rows
    partial_value = jnp.dot(local_x, weight, preferred_element_type=jnp.float32)
    preact = row_reduce_scatter(partial_value) + bias
    my_cot = lax.dynamic_slice_in_dim(cotangent, first_row, my_rows, 0)
    hidden, my_grad = activate(preact, my_cot)
    full_grad = row_all_gather(my_grad)
    grad_tokens = lax.psum_scatter(
        lax.dot_general(
            full_grad, weight, (((1,), (1,)), ((), ())), preferred_element_type=jnp.float32
        ),
        "col",
        scatter_dimension=0,
        tiled=True,
    ).astype(jnp.bfloat16)
    grad_weight = outer_product_sum(local_x.T, full_grad)
    grad_bias = jnp.sum(full_grad.astype(jnp.float32), axis=0)
    return (hidden, grad_tokens, grad_weight, grad_bias)


def solution(mesh):
    placed = (P("col", "row"), P("row", "col"), P("col"), P(None, "col"))
    return jax.shard_map(
        body,
        mesh=mesh,
        in_specs=placed,
        out_specs=(P("row", "col"), P("col", "row"), P("row", "col"), P("col")),
        check_vma=False,
    )
```

```python
import math

import jax
import jax.numpy as jnp
from jax import lax
from jax.experimental import pallas as pl
from jax.experimental.pallas import tpu as pltpu
from jax.sharding import PartitionSpec as P


def activate(preact, cotangent):
    normal_cdf = 0.5 * (1.0 + jax.scipy.special.erf(preact / math.sqrt(2.0)))
    normal_pdf = jnp.exp(-0.5 * preact * preact) / math.sqrt(2.0 * math.pi)
    hidden = (preact * normal_cdf).astype(jnp.bfloat16)
    grad_pre = (cotangent.astype(jnp.float32) * (normal_cdf + preact * normal_pdf)).astype(
        jnp.bfloat16
    )
    return (hidden, grad_pre)


def _outer_kernel(xt_ref, g_ref, o_ref):
    o_ref[...] = jnp.dot(xt_ref[...], g_ref[...], preferred_element_type=jnp.float32).astype(
        o_ref.dtype
    )


def outer_product_sum(xt, g, block_m=768, block_n=3072):
    m, k = xt.shape
    n = g.shape[1]
    block_m = min(block_m, m)
    block_n = min(block_n, n)
    return pl.pallas_call(
        _outer_kernel,
        grid=(n // block_n, m // block_m),
        in_specs=[
            pl.BlockSpec((block_m, k), lambda j, i: (i, 0)),
            pl.BlockSpec((k, block_n), lambda j, i: (0, j)),
        ],
        out_specs=pl.BlockSpec((block_m, block_n), lambda j, i: (i, j)),
        out_shape=jax.ShapeDtypeStruct((m, n), jnp.bfloat16),
        cost_estimate=pl.CostEstimate(
            flops=2 * m * n * k, transcendentals=0, bytes_accessed=2 * (m * k + k * n + m * n)
        ),
    )(xt, g)


def _swap(value, axis, flip):
    size = lax.axis_size(axis)
    return lax.ppermute(value, axis, [(i, i ^ flip) for i in range(size)])


def _pick(index, blocks):
    return lax.dynamic_index_in_dim(blocks, index, axis=0, keepdims=False)


def _halves(value):
    cols = value.shape[1]
    if cols % 256:
        return [value]
    return [value[:, : cols // 2], value[:, cols // 2 :]]


def _bit_orders(n):
    order = list(range(n.bit_length() - 1))
    return [order, order[::-1]]


def row_reduce_scatter(partial, axis="row"):
    n = lax.axis_size(axis)
    if n & (n - 1):
        return lax.psum_scatter(partial, axis, scatter_dimension=0, tiled=True)
    levels = n.bit_length() - 1
    r = lax.axis_index(axis)
    m = partial.shape[0] // n
    outs = []
    for half, order in zip(_halves(partial), _bit_orders(n)):
        cur = half.reshape([2] * levels + [m, half.shape[1]])
        bits = list(range(levels))[::-1]
        for bit in order:
            mine = (r >> bit) & 1
            t = jnp.moveaxis(cur, bits.index(bit), 0)
            sent = _swap(_pick(1 - mine, t).astype(jnp.bfloat16), axis, 1 << bit)
            cur = _pick(mine, t) + sent.astype(jnp.float32)
            bits.remove(bit)
        outs.append(cur.reshape(m, half.shape[1]))
    return jnp.concatenate(outs, axis=1)


def _pair(mine, theirs, bit):
    first = jnp.where(bit == 0, mine, theirs)
    second = jnp.where(bit == 0, theirs, mine)
    return jnp.stack([first, second], axis=0)


def row_all_gather(block, axis="row"):
    n = lax.axis_size(axis)
    if n & (n - 1):
        return lax.all_gather(block, axis, axis=0, tiled=True)
    levels = n.bit_length() - 1
    r = lax.axis_index(axis)
    m = block.shape[0]
    outs = []
    for half, order in zip(_halves(block), _bit_orders(n)):
        cur = half
        bits = []
        for bit in order:
            cur = _pair(cur, _swap(cur, axis, 1 << bit), (r >> bit) & 1)
            bits.insert(0, bit)
        perm = sorted(range(levels), key=lambda j: -bits[j])
        cur = jnp.transpose(cur, perm + [levels, levels + 1])
        outs.append(cur.reshape(n * m, half.shape[1]))
    return jnp.concatenate(outs, axis=1)


def col_all_gather(block, axis="col"):
    n = lax.axis_size(axis)
    if n % 2:
        return lax.all_gather(block, axis, axis=0, tiled=True)
    groups = [list(range(k, n, 2)) for k in range(2)]
    mine = lax.all_gather(block, axis, axis_index_groups=groups)
    both = _pair(mine, _swap(mine, axis, 1), lax.axis_index(axis) % 2)
    return jnp.swapaxes(both, 0, 1).reshape(n * block.shape[0], block.shape[1])


def body(tokens, weight, bias, cotangent):
    local_x = col_all_gather(tokens)
    my_rows = local_x.shape[0] // lax.axis_size("row")
    first_row = lax.axis_index("row") * my_rows
    partial_value = jnp.dot(local_x, weight, preferred_element_type=jnp.float32)
    preact = row_reduce_scatter(partial_value) + bias
    my_cot = lax.dynamic_slice_in_dim(cotangent, first_row, my_rows, 0)
    hidden, my_grad = activate(preact, my_cot)
    full_grad = row_all_gather(my_grad)
    grad_tokens = lax.psum_scatter(
        lax.dot_general(
            full_grad, weight, (((1,), (1,)), ((), ())), preferred_element_type=jnp.float32
        ),
        "col",
        scatter_dimension=0,
        tiled=True,
    ).astype(jnp.bfloat16)
    grad_weight = outer_product_sum(local_x.T, full_grad)
    grad_bias = jnp.sum(full_grad.astype(jnp.float32), axis=0)
    return (hidden, grad_tokens, grad_weight, grad_bias)


def solution(mesh):
    placed = (P("col", "row"), P("row", "col"), P("col"), P(None, "col"))
    return jax.shard_map(
        body,
        mesh=mesh,
        in_specs=placed,
        out_specs=(P("row", "col"), P("col", "row"), P("row", "col"), P("col")),
        check_vma=False,
    )
```

```python
import math

import jax
import jax.numpy as jnp
from jax import lax
from jax.experimental import pallas as pl
from jax.experimental.pallas import tpu as pltpu
from jax.sharding import PartitionSpec as P


def activate(preact, cotangent):
    normal_cdf = 0.5 * (1.0 + jax.scipy.special.erf(preact / math.sqrt(2.0)))
    normal_pdf = jnp.exp(-0.5 * preact * preact) / math.sqrt(2.0 * math.pi)
    hidden = (preact * normal_cdf).astype(jnp.bfloat16)
    grad_pre = (cotangent.astype(jnp.float32) * (normal_cdf + preact * normal_pdf)).astype(
        jnp.bfloat16
    )
    return (hidden, grad_pre)


def _outer_kernel(xt_ref, g_ref, o_ref):
    o_ref[...] = jnp.dot(xt_ref[...], g_ref[...], preferred_element_type=jnp.float32).astype(
        o_ref.dtype
    )


def outer_product_sum(xt, g, block_m=768, block_n=3072):
    m, k = xt.shape
    n = g.shape[1]
    block_m = min(block_m, m)
    block_n = min(block_n, n)
    return pl.pallas_call(
        _outer_kernel,
        grid=(n // block_n, m // block_m),
        in_specs=[
            pl.BlockSpec((block_m, k), lambda j, i: (i, 0)),
            pl.BlockSpec((k, block_n), lambda j, i: (0, j)),
        ],
        out_specs=pl.BlockSpec((block_m, block_n), lambda j, i: (i, j)),
        out_shape=jax.ShapeDtypeStruct((m, n), jnp.bfloat16),
        cost_estimate=pl.CostEstimate(
            flops=2 * m * n * k, transcendentals=0, bytes_accessed=2 * (m * k + k * n + m * n)
        ),
    )(xt, g)


def _swap(value, axis, flip):
    size = lax.axis_size(axis)
    return lax.ppermute(value, axis, [(i, i ^ flip) for i in range(size)])


def _pick(index, blocks):
    return lax.dynamic_index_in_dim(blocks, index, axis=0, keepdims=False)


def _halves(value):
    cols = value.shape[1]
    if cols % 256:
        return [value]
    return [value[:, : cols // 2], value[:, cols // 2 :]]


def _bit_orders(n):
    order = list(range(n.bit_length() - 1))
    return [order, order[::-1]]


def row_reduce_scatter(partial, axis="row"):
    n = lax.axis_size(axis)
    if n & (n - 1):
        return lax.psum_scatter(partial, axis, scatter_dimension=0, tiled=True)
    levels = n.bit_length() - 1
    r = lax.axis_index(axis)
    m = partial.shape[0] // n
    outs = []
    for half, order in zip(_halves(partial), _bit_orders(n)):
        cur = half.reshape([2] * levels + [m, half.shape[1]])
        bits = list(range(levels))[::-1]
        for bit in order:
            mine = (r >> bit) & 1
            t = jnp.moveaxis(cur, bits.index(bit), 0)
            sent = _swap(_pick(1 - mine, t).astype(jnp.bfloat16), axis, 1 << bit)
            cur = _pick(mine, t) + sent.astype(jnp.float32)
            bits.remove(bit)
        outs.append(cur.reshape(m, half.shape[1]))
    return jnp.concatenate(outs, axis=1)


def _pair(mine, theirs, bit):
    first = jnp.where(bit == 0, mine, theirs)
    second = jnp.where(bit == 0, theirs, mine)
    return jnp.stack([first, second], axis=0)


def row_all_gather(block, axis="row"):
    n = lax.axis_size(axis)
    if n & (n - 1):
        return lax.all_gather(block, axis, axis=0, tiled=True)
    levels = n.bit_length() - 1
    r = lax.axis_index(axis)
    m = block.shape[0]
    outs = []
    for half, order in zip(_halves(block), _bit_orders(n)):
        cur = half
        bits = []
        for bit in order:
            cur = _pair(cur, _swap(cur, axis, 1 << bit), (r >> bit) & 1)
            bits.insert(0, bit)
        perm = sorted(range(levels), key=lambda j: -bits[j])
        cur = jnp.transpose(cur, perm + [levels, levels + 1])
        outs.append(cur.reshape(n * m, half.shape[1]))
    return jnp.concatenate(outs, axis=1)


def col_all_gather(block, axis="col"):
    n = lax.axis_size(axis)
    if n % 2:
        return lax.all_gather(block, axis, axis=0, tiled=True)
    groups = [list(range(k, n, 2)) for k in range(2)]
    mine = lax.all_gather(block, axis, axis_index_groups=groups)
    both = _pair(mine, _swap(mine, axis, 1), lax.axis_index(axis) % 2)
    return jnp.swapaxes(both, 0, 1).reshape(n * block.shape[0], block.shape[1])


def col_reduce_scatter(partial, axis="col"):
    n = lax.axis_size(axis)
    if n % 2:
        return lax.psum_scatter(partial, axis, scatter_dimension=0, tiled=True)
    m = partial.shape[0] // n
    k = lax.axis_index(axis) % 2
    by_core = jnp.swapaxes(partial.reshape(n // 2, 2, m, partial.shape[1]), 0, 1)
    chip = _pick(k, by_core) + _swap(_pick(1 - k, by_core), axis, 1)
    groups = [list(range(j, n, 2)) for j in range(2)]
    return lax.psum_scatter(
        chip.reshape(n // 2 * m, partial.shape[1]),
        axis,
        scatter_dimension=0,
        tiled=True,
        axis_index_groups=groups,
    )


def body(tokens, weight, bias, cotangent):
    local_x = col_all_gather(tokens)
    my_rows = local_x.shape[0] // lax.axis_size("row")
    first_row = lax.axis_index("row") * my_rows
    partial_value = jnp.dot(local_x, weight, preferred_element_type=jnp.float32)
    preact = row_reduce_scatter(partial_value) + bias
    my_cot = lax.dynamic_slice_in_dim(cotangent, first_row, my_rows, 0)
    hidden, my_grad = activate(preact, my_cot)
    full_grad = row_all_gather(my_grad)
    grad_tokens = col_reduce_scatter(
        lax.dot_general(
            full_grad, weight, (((1,), (1,)), ((), ())), preferred_element_type=jnp.float32
        )
    ).astype(jnp.bfloat16)
    grad_weight = outer_product_sum(local_x.T, full_grad)
    grad_bias = jnp.sum(full_grad.astype(jnp.float32), axis=0)
    return (hidden, grad_tokens, grad_weight, grad_bias)


def solution(mesh):
    placed = (P("col", "row"), P("row", "col"), P("col"), P(None, "col"))
    return jax.shard_map(
        body,
        mesh=mesh,
        in_specs=placed,
        out_specs=(P("row", "col"), P("col", "row"), P("row", "col"), P("col")),
        check_vma=False,
    )
```

```python
import math

import jax
import jax.numpy as jnp
from jax import lax
from jax.experimental import pallas as pl
from jax.experimental.pallas import tpu as pltpu
from jax.sharding import PartitionSpec as P


def activate(preact, cotangent):
    normal_cdf = 0.5 * (1.0 + jax.scipy.special.erf(preact / math.sqrt(2.0)))
    normal_pdf = jnp.exp(-0.5 * preact * preact) / math.sqrt(2.0 * math.pi)
    hidden = (preact * normal_cdf).astype(jnp.bfloat16)
    grad_pre = (cotangent.astype(jnp.float32) * (normal_cdf + preact * normal_pdf)).astype(
        jnp.bfloat16
    )
    return (hidden, grad_pre)


def _outer_kernel(xt_ref, g_ref, o_ref):
    o_ref[...] = jnp.dot(xt_ref[...], g_ref[...], preferred_element_type=jnp.float32).astype(
        o_ref.dtype
    )


def outer_product_sum(xt, g, block_m=768, block_n=3072):
    m, k = xt.shape
    n = g.shape[1]
    block_m = min(block_m, m)
    block_n = min(block_n, n)
    return pl.pallas_call(
        _outer_kernel,
        grid=(n // block_n, m // block_m),
        in_specs=[
            pl.BlockSpec((block_m, k), lambda j, i: (i, 0)),
            pl.BlockSpec((k, block_n), lambda j, i: (0, j)),
        ],
        out_specs=pl.BlockSpec((block_m, block_n), lambda j, i: (i, j)),
        out_shape=jax.ShapeDtypeStruct((m, n), jnp.bfloat16),
        cost_estimate=pl.CostEstimate(
            flops=2 * m * n * k, transcendentals=0, bytes_accessed=2 * (m * k + k * n + m * n)
        ),
    )(xt, g)


def _swap(value, axis, flip):
    size = lax.axis_size(axis)
    return lax.ppermute(value, axis, [(i, i ^ flip) for i in range(size)])


def _pick(index, blocks):
    return lax.dynamic_index_in_dim(blocks, index, axis=0, keepdims=False)


def _halves(value):
    cols = value.shape[1]
    if cols % 256:
        return [value]
    return [value[:, : cols // 2], value[:, cols // 2 :]]


def _bit_orders(n):
    order = list(range(n.bit_length() - 1))
    return [order, order[::-1]]


def row_reduce_scatter(partial, axis="row"):
    n = lax.axis_size(axis)
    if n & (n - 1):
        return lax.psum_scatter(partial, axis, scatter_dimension=0, tiled=True)
    levels = n.bit_length() - 1
    r = lax.axis_index(axis)
    m = partial.shape[0] // n
    outs = []
    for half, order in zip(_halves(partial), _bit_orders(n)):
        cur = half.reshape([2] * levels + [m, half.shape[1]])
        bits = list(range(levels))[::-1]
        for bit in order:
            mine = (r >> bit) & 1
            t = jnp.moveaxis(cur, bits.index(bit), 0)
            sent = _swap(_pick(1 - mine, t).astype(jnp.bfloat16), axis, 1 << bit)
            cur = _pick(mine, t) + sent.astype(jnp.float32)
            bits.remove(bit)
        outs.append(cur.reshape(m, half.shape[1]))
    return jnp.concatenate(outs, axis=1)


def _pair(mine, theirs, bit):
    first = jnp.where(bit == 0, mine, theirs)
    second = jnp.where(bit == 0, theirs, mine)
    return jnp.stack([first, second], axis=0)


def row_all_gather(block, axis="row"):
    n = lax.axis_size(axis)
    if n & (n - 1):
        return lax.all_gather(block, axis, axis=0, tiled=True)
    levels = n.bit_length() - 1
    r = lax.axis_index(axis)
    m = block.shape[0]
    outs = []
    for half, order in zip(_halves(block), _bit_orders(n)):
        cur = half
        bits = []
        for bit in order:
            cur = _pair(cur, _swap(cur, axis, 1 << bit), (r >> bit) & 1)
            bits.insert(0, bit)
        perm = sorted(range(levels), key=lambda j: -bits[j])
        cur = jnp.transpose(cur, perm + [levels, levels + 1])
        outs.append(cur.reshape(n * m, half.shape[1]))
    return jnp.concatenate(outs, axis=1)


def col_all_gather(block, axis="col"):
    n = lax.axis_size(axis)
    if n % 2:
        return lax.all_gather(block, axis, axis=0, tiled=True)
    groups = [list(range(k, n, 2)) for k in range(2)]
    mine = lax.all_gather(block, axis, axis_index_groups=groups)
    both = _pair(mine, _swap(mine, axis, 1), lax.axis_index(axis) % 2)
    return jnp.swapaxes(both, 0, 1).reshape(n * block.shape[0], block.shape[1])


def col_reduce_scatter(partial, axis="col"):
    n = lax.axis_size(axis)
    if n % 2:
        return lax.psum_scatter(partial, axis, scatter_dimension=0, tiled=True)
    m = partial.shape[0] // n
    k = lax.axis_index(axis) % 2
    by_core = jnp.swapaxes(partial.reshape(n // 2, 2, m, partial.shape[1]), 0, 1)
    chip = _pick(k, by_core) + _swap(_pick(1 - k, by_core), axis, 1)
    chips = n // 2
    z = lax.axis_index(axis) // 2
    total = _pick(z, chip)
    for d in range(1, chips):
        pairs = [(2 * i + j, 2 * ((i + d) % chips) + j) for i in range(chips) for j in range(2)]
        total = total + lax.ppermute(_pick((z + d) % chips, chip), axis, pairs)
    return total


def body(tokens, weight, bias, cotangent):
    local_x = col_all_gather(tokens)
    my_rows = local_x.shape[0] // lax.axis_size("row")
    first_row = lax.axis_index("row") * my_rows
    partial_value = jnp.dot(local_x, weight, preferred_element_type=jnp.float32)
    preact = row_reduce_scatter(partial_value) + bias
    my_cot = lax.dynamic_slice_in_dim(cotangent, first_row, my_rows, 0)
    hidden, my_grad = activate(preact, my_cot)
    full_grad = row_all_gather(my_grad)
    grad_tokens = col_reduce_scatter(
        lax.dot_general(
            full_grad, weight, (((1,), (1,)), ((), ())), preferred_element_type=jnp.float32
        )
    ).astype(jnp.bfloat16)
    grad_weight = outer_product_sum(local_x.T, full_grad)
    grad_bias = jnp.sum(full_grad.astype(jnp.float32), axis=0)
    return (hidden, grad_tokens, grad_weight, grad_bias)


def solution(mesh):
    placed = (P("col", "row"), P("row", "col"), P("col"), P(None, "col"))
    return jax.shard_map(
        body,
        mesh=mesh,
        in_specs=placed,
        out_specs=(P("row", "col"), P("col", "row"), P("row", "col"), P("col")),
        check_vma=False,
    )
```

```python
import math

import jax
import jax.numpy as jnp
from jax import lax
from jax.experimental import pallas as pl
from jax.experimental.pallas import tpu as pltpu
from jax.sharding import PartitionSpec as P


def activate(preact, cotangent):
    normal_cdf = 0.5 * (1.0 + jax.scipy.special.erf(preact / math.sqrt(2.0)))
    normal_pdf = jnp.exp(-0.5 * preact * preact) / math.sqrt(2.0 * math.pi)
    hidden = (preact * normal_cdf).astype(jnp.bfloat16)
    grad_pre = (cotangent.astype(jnp.float32) * (normal_cdf + preact * normal_pdf)).astype(
        jnp.bfloat16
    )
    return (hidden, grad_pre)


def _outer_kernel(xt_ref, g_ref, o_ref):
    o_ref[...] = jnp.dot(xt_ref[...], g_ref[...], preferred_element_type=jnp.float32).astype(
        o_ref.dtype
    )


def outer_product_sum(xt, g, block_m=768, block_n=3072):
    m, k = xt.shape
    n = g.shape[1]
    block_m = min(block_m, m)
    block_n = min(block_n, n)
    return pl.pallas_call(
        _outer_kernel,
        grid=(n // block_n, m // block_m),
        in_specs=[
            pl.BlockSpec((block_m, k), lambda j, i: (i, 0)),
            pl.BlockSpec((k, block_n), lambda j, i: (0, j)),
        ],
        out_specs=pl.BlockSpec((block_m, block_n), lambda j, i: (i, j)),
        out_shape=jax.ShapeDtypeStruct((m, n), jnp.bfloat16),
        cost_estimate=pl.CostEstimate(
            flops=2 * m * n * k, transcendentals=0, bytes_accessed=2 * (m * k + k * n + m * n)
        ),
    )(xt, g)


def _swap(value, axis, flip):
    size = lax.axis_size(axis)
    return lax.ppermute(value, axis, [(i, i ^ flip) for i in range(size)])


def _pick(index, blocks):
    return lax.dynamic_index_in_dim(blocks, index, axis=0, keepdims=False)


def _halves(value):
    cols = value.shape[1]
    if cols % 256:
        return [value]
    return [value[:, : cols // 2], value[:, cols // 2 :]]


def _bit_orders(n):
    order = list(range(n.bit_length() - 1))
    return [order, order[::-1]]


def row_reduce_scatter(partial, axis="row"):
    n = lax.axis_size(axis)
    if n & (n - 1):
        return lax.psum_scatter(partial, axis, scatter_dimension=0, tiled=True)
    levels = n.bit_length() - 1
    r = lax.axis_index(axis)
    m = partial.shape[0] // n
    outs = []
    for half, order in zip(_halves(partial), _bit_orders(n)):
        cur = half.reshape([2] * levels + [m, half.shape[1]])
        bits = list(range(levels))[::-1]
        for bit in order:
            mine = (r >> bit) & 1
            t = jnp.moveaxis(cur, bits.index(bit), 0)
            sent = _swap(_pick(1 - mine, t).astype(jnp.bfloat16), axis, 1 << bit)
            cur = _pick(mine, t) + sent.astype(jnp.float32)
            bits.remove(bit)
        outs.append(cur.reshape(m, half.shape[1]))
    return jnp.concatenate(outs, axis=1)


def _pair(mine, theirs, bit):
    first = jnp.where(bit == 0, mine, theirs)
    second = jnp.where(bit == 0, theirs, mine)
    return jnp.stack([first, second], axis=0)


def row_all_gather(block, axis="row"):
    n = lax.axis_size(axis)
    if n & (n - 1):
        return lax.all_gather(block, axis, axis=0, tiled=True)
    levels = n.bit_length() - 1
    r = lax.axis_index(axis)
    m = block.shape[0]
    outs = []
    for half, order in zip(_halves(block), _bit_orders(n)):
        cur = half
        bits = []
        for bit in order:
            cur = _pair(cur, _swap(cur, axis, 1 << bit), (r >> bit) & 1)
            bits.insert(0, bit)
        perm = sorted(range(levels), key=lambda j: -bits[j])
        cur = jnp.transpose(cur, perm + [levels, levels + 1])
        outs.append(cur.reshape(n * m, half.shape[1]))
    return jnp.concatenate(outs, axis=1)


def col_all_gather(block, axis="col"):
    n = lax.axis_size(axis)
    if n % 2:
        return lax.all_gather(block, axis, axis=0, tiled=True)
    groups = [list(range(k, n, 2)) for k in range(2)]
    mine = lax.all_gather(block, axis, axis_index_groups=groups)
    both = _pair(mine, _swap(mine, axis, 1), lax.axis_index(axis) % 2)
    return jnp.swapaxes(both, 0, 1).reshape(n * block.shape[0], block.shape[1])


def col_reduce_scatter(partial, axis="col"):
    n = lax.axis_size(axis)
    if n % 2:
        return lax.psum_scatter(partial, axis, scatter_dimension=0, tiled=True)
    m = partial.shape[0] // n
    k = lax.axis_index(axis) % 2
    by_core = jnp.swapaxes(partial.reshape(n // 2, 2, m, partial.shape[1]), 0, 1)
    chip = _pick(k, by_core) + _swap(_pick(1 - k, by_core), axis, 1)
    chips = n // 2
    z = lax.axis_index(axis) // 2
    if chips & (chips - 1):
        total = _pick(z, chip)
        for d in range(1, chips):
            pairs = [(2 * i + j, 2 * ((i + d) % chips) + j) for i in range(chips) for j in range(2)]
            total = total + lax.ppermute(_pick((z + d) % chips, chip), axis, pairs)
        return total
    levels = chips.bit_length() - 1
    cur = chip.reshape([2] * levels + [m, partial.shape[1]])
    bits = list(range(levels))[::-1]
    for bit in range(levels):
        mine = (z >> bit) & 1
        t = jnp.moveaxis(cur, bits.index(bit), 0)
        cur = _pick(mine, t) + _swap(_pick(1 - mine, t), axis, 2 << bit)
        bits.remove(bit)
    return cur.reshape(m, partial.shape[1])


def body(tokens, weight, bias, cotangent):
    local_x = col_all_gather(tokens)
    my_rows = local_x.shape[0] // lax.axis_size("row")
    first_row = lax.axis_index("row") * my_rows
    partial_value = jnp.dot(local_x, weight, preferred_element_type=jnp.float32)
    preact = row_reduce_scatter(partial_value) + bias
    my_cot = lax.dynamic_slice_in_dim(cotangent, first_row, my_rows, 0)
    hidden, my_grad = activate(preact, my_cot)
    full_grad = row_all_gather(my_grad)
    grad_tokens = col_reduce_scatter(
        lax.dot_general(
            full_grad, weight, (((1,), (1,)), ((), ())), preferred_element_type=jnp.float32
        )
    ).astype(jnp.bfloat16)
    grad_weight = outer_product_sum(local_x.T, full_grad)
    grad_bias = jnp.sum(full_grad.astype(jnp.float32), axis=0)
    return (hidden, grad_tokens, grad_weight, grad_bias)


def solution(mesh):
    placed = (P("col", "row"), P("row", "col"), P("col"), P(None, "col"))
    return jax.shard_map(
        body,
        mesh=mesh,
        in_specs=placed,
        out_specs=(P("row", "col"), P("col", "row"), P("row", "col"), P("col")),
        check_vma=False,
    )
```

```python
import math

import jax
import jax.numpy as jnp
from jax import lax
from jax.experimental import pallas as pl
from jax.experimental.pallas import tpu as pltpu
from jax.sharding import PartitionSpec as P


def activate(preact, cotangent):
    normal_cdf = 0.5 * (1.0 + jax.scipy.special.erf(preact / math.sqrt(2.0)))
    normal_pdf = jnp.exp(-0.5 * preact * preact) / math.sqrt(2.0 * math.pi)
    hidden = (preact * normal_cdf).astype(jnp.bfloat16)
    grad_pre = (cotangent.astype(jnp.float32) * (normal_cdf + preact * normal_pdf)).astype(
        jnp.bfloat16
    )
    return (hidden, grad_pre)


def _outer_kernel(xt_ref, g_ref, o_ref):
    o_ref[...] = jnp.dot(xt_ref[...], g_ref[...], preferred_element_type=jnp.float32).astype(
        o_ref.dtype
    )


def outer_product_sum(xt, g, block_m=768, block_n=3072):
    m, k = xt.shape
    n = g.shape[1]
    block_m = min(block_m, m)
    block_n = min(block_n, n)
    return pl.pallas_call(
        _outer_kernel,
        grid=(n // block_n, m // block_m),
        in_specs=[
            pl.BlockSpec((block_m, k), lambda j, i: (i, 0)),
            pl.BlockSpec((k, block_n), lambda j, i: (0, j)),
        ],
        out_specs=pl.BlockSpec((block_m, block_n), lambda j, i: (i, j)),
        out_shape=jax.ShapeDtypeStruct((m, n), jnp.bfloat16),
        cost_estimate=pl.CostEstimate(
            flops=2 * m * n * k, transcendentals=0, bytes_accessed=2 * (m * k + k * n + m * n)
        ),
    )(xt, g)


def _swap(value, axis, flip):
    size = lax.axis_size(axis)
    return lax.ppermute(value, axis, [(i, i ^ flip) for i in range(size)])


def _pick(index, blocks):
    return lax.dynamic_index_in_dim(blocks, index, axis=0, keepdims=False)


def _halves(value):
    cols = value.shape[1]
    if cols % 256:
        return [value]
    return [value[:, : cols // 2], value[:, cols // 2 :]]


def _bit_orders(n):
    order = list(range(n.bit_length() - 1))
    return [order, order[::-1]]


def row_reduce_scatter(partial, axis="row"):
    n = lax.axis_size(axis)
    if n & (n - 1):
        return lax.psum_scatter(partial, axis, scatter_dimension=0, tiled=True)
    levels = n.bit_length() - 1
    r = lax.axis_index(axis)
    m = partial.shape[0] // n
    outs = []
    for half, order in zip(_halves(partial), _bit_orders(n)):
        cur = half.reshape([2] * levels + [m, half.shape[1]])
        bits = list(range(levels))[::-1]
        for bit in order:
            mine = (r >> bit) & 1
            t = jnp.moveaxis(cur, bits.index(bit), 0)
            sent = _swap(_pick(1 - mine, t).astype(jnp.bfloat16), axis, 1 << bit)
            cur = _pick(mine, t) + sent.astype(jnp.float32)
            bits.remove(bit)
        outs.append(cur.reshape(m, half.shape[1]))
    return jnp.concatenate(outs, axis=1)


def _pair(mine, theirs, bit):
    first = jnp.where(bit == 0, mine, theirs)
    second = jnp.where(bit == 0, theirs, mine)
    return jnp.stack([first, second], axis=0)


def row_all_gather(block, axis="row"):
    n = lax.axis_size(axis)
    if n & (n - 1):
        return lax.all_gather(block, axis, axis=0, tiled=True)
    levels = n.bit_length() - 1
    r = lax.axis_index(axis)
    m = block.shape[0]
    outs = []
    for half, order in zip(_halves(block), _bit_orders(n)):
        cur = half
        bits = []
        for bit in order:
            cur = _pair(cur, _swap(cur, axis, 1 << bit), (r >> bit) & 1)
            bits.insert(0, bit)
        perm = sorted(range(levels), key=lambda j: -bits[j])
        cur = jnp.transpose(cur, perm + [levels, levels + 1])
        outs.append(cur.reshape(n * m, half.shape[1]))
    return jnp.concatenate(outs, axis=1)


def col_all_gather(block, axis="col"):
    n = lax.axis_size(axis)
    if n % 2:
        return lax.all_gather(block, axis, axis=0, tiled=True)
    groups = [list(range(k, n, 2)) for k in range(2)]
    mine = lax.all_gather(block, axis, axis_index_groups=groups)
    both = _pair(mine, _swap(mine, axis, 1), lax.axis_index(axis) % 2)
    return jnp.swapaxes(both, 0, 1).reshape(n * block.shape[0], block.shape[1])


def col_reduce_scatter(partial, hold, axis="col"):
    n = lax.axis_size(axis)
    if n % 2:
        return lax.psum_scatter(partial, axis, scatter_dimension=0, tiled=True), hold
    m = partial.shape[0] // n
    k = lax.axis_index(axis) % 2
    by_core = jnp.swapaxes(partial.reshape(n // 2, 2, m, partial.shape[1]), 0, 1)
    chip = _pick(k, by_core) + _swap(_pick(1 - k, by_core), axis, 1)
    chips = n // 2
    z = lax.axis_index(axis) // 2
    if chips & (chips - 1):
        total = _pick(z, chip)
        for d in range(1, chips):
            pairs = [(2 * i + j, 2 * ((i + d) % chips) + j) for i in range(chips) for j in range(2)]
            total = total + lax.ppermute(_pick((z + d) % chips, chip), axis, pairs)
        return total, hold
    levels = chips.bit_length() - 1
    cur = chip.reshape([2] * levels + [m, partial.shape[1]])
    bits = list(range(levels))[::-1]
    for bit in range(levels):
        mine = (z >> bit) & 1
        t = jnp.moveaxis(cur, bits.index(bit), 0)
        cur = _pick(mine, t) + _swap(_pick(1 - mine, t), axis, 2 << bit)
        bits.remove(bit)
        if bit == 0:
            cur, hold = lax.optimization_barrier((cur, hold))
    return cur.reshape(m, partial.shape[1]), hold


def body(tokens, weight, bias, cotangent):
    local_x = col_all_gather(tokens)
    my_rows = local_x.shape[0] // lax.axis_size("row")
    first_row = lax.axis_index("row") * my_rows
    partial_value = jnp.dot(local_x, weight, preferred_element_type=jnp.float32)
    preact = row_reduce_scatter(partial_value) + bias
    my_cot = lax.dynamic_slice_in_dim(cotangent, first_row, my_rows, 0)
    hidden, my_grad = activate(preact, my_cot)
    full_grad = row_all_gather(my_grad)
    grad_weight = outer_product_sum(local_x.T, full_grad)
    grad_tokens, grad_weight = col_reduce_scatter(
        lax.dot_general(
            full_grad, weight, (((1,), (1,)), ((), ())), preferred_element_type=jnp.float32
        ),
        grad_weight,
    )
    grad_tokens = grad_tokens.astype(jnp.bfloat16)
    grad_bias = jnp.sum(full_grad.astype(jnp.float32), axis=0)
    return (hidden, grad_tokens, grad_weight, grad_bias)


def solution(mesh):
    placed = (P("col", "row"), P("row", "col"), P("col"), P(None, "col"))
    return jax.shard_map(
        body,
        mesh=mesh,
        in_specs=placed,
        out_specs=(P("row", "col"), P("col", "row"), P("row", "col"), P("col")),
        check_vma=False,
    )
```

```python
import math

import jax
import jax.numpy as jnp
from jax import lax
from jax.experimental import pallas as pl
from jax.experimental.pallas import tpu as pltpu
from jax.sharding import PartitionSpec as P


def activate(preact, cotangent):
    normal_cdf = 0.5 * (1.0 + jax.scipy.special.erf(preact / math.sqrt(2.0)))
    normal_pdf = jnp.exp(-0.5 * preact * preact) / math.sqrt(2.0 * math.pi)
    hidden = (preact * normal_cdf).astype(jnp.bfloat16)
    grad_pre = (cotangent.astype(jnp.float32) * (normal_cdf + preact * normal_pdf)).astype(
        jnp.bfloat16
    )
    return (hidden, grad_pre)


def _outer_kernel(xt_ref, g_ref, o_ref):
    o_ref[...] = jnp.dot(xt_ref[...], g_ref[...], preferred_element_type=jnp.float32).astype(
        o_ref.dtype
    )


def outer_product_sum(xt, g, block_m=768, block_n=3072):
    m, k = xt.shape
    n = g.shape[1]
    block_m = min(block_m, m)
    block_n = min(block_n, n)
    return pl.pallas_call(
        _outer_kernel,
        grid=(n // block_n, m // block_m),
        in_specs=[
            pl.BlockSpec((block_m, k), lambda j, i: (i, 0)),
            pl.BlockSpec((k, block_n), lambda j, i: (0, j)),
        ],
        out_specs=pl.BlockSpec((block_m, block_n), lambda j, i: (i, j)),
        out_shape=jax.ShapeDtypeStruct((m, n), jnp.bfloat16),
        cost_estimate=pl.CostEstimate(
            flops=2 * m * n * k, transcendentals=0, bytes_accessed=2 * (m * k + k * n + m * n)
        ),
    )(xt, g)


def _swap(value, axis, flip):
    size = lax.axis_size(axis)
    return lax.ppermute(value, axis, [(i, i ^ flip) for i in range(size)])


def _pick(index, blocks):
    return lax.dynamic_index_in_dim(blocks, index, axis=0, keepdims=False)


def _halves(value):
    cols = value.shape[1]
    if cols % 256:
        return [value]
    return [value[:, : cols // 2], value[:, cols // 2 :]]


def _bit_orders(n):
    order = list(range(n.bit_length() - 1))
    return [order, order[::-1]]


def row_reduce_scatter(partial, axis="row"):
    n = lax.axis_size(axis)
    if n & (n - 1):
        return lax.psum_scatter(partial, axis, scatter_dimension=0, tiled=True)
    levels = n.bit_length() - 1
    r = lax.axis_index(axis)
    m = partial.shape[0] // n
    outs = []
    for half, order in zip(_halves(partial), _bit_orders(n)):
        cur = half.reshape([2] * levels + [m, half.shape[1]])
        bits = list(range(levels))[::-1]
        for bit in order:
            mine = (r >> bit) & 1
            t = jnp.moveaxis(cur, bits.index(bit), 0)
            sent = _swap(_pick(1 - mine, t).astype(jnp.bfloat16), axis, 1 << bit)
            cur = _pick(mine, t) + sent.astype(jnp.float32)
            bits.remove(bit)
        outs.append(cur.reshape(m, half.shape[1]))
    return jnp.concatenate(outs, axis=1)


def _pair(mine, theirs, bit):
    first = jnp.where(bit == 0, mine, theirs)
    second = jnp.where(bit == 0, theirs, mine)
    return jnp.stack([first, second], axis=0)


def row_all_gather(block, axis="row"):
    n = lax.axis_size(axis)
    if n & (n - 1):
        return lax.all_gather(block, axis, axis=0, tiled=True)
    levels = n.bit_length() - 1
    r = lax.axis_index(axis)
    m = block.shape[0]
    outs = []
    for half, order in zip(_halves(block), _bit_orders(n)):
        cur = half
        bits = []
        for bit in order:
            cur = _pair(cur, _swap(cur, axis, 1 << bit), (r >> bit) & 1)
            bits.insert(0, bit)
        perm = sorted(range(levels), key=lambda j: -bits[j])
        cur = jnp.transpose(cur, perm + [levels, levels + 1])
        outs.append(cur.reshape(n * m, half.shape[1]))
    return jnp.concatenate(outs, axis=1)


def col_all_gather(block, axis="col"):
    n = lax.axis_size(axis)
    if n % 2:
        return lax.all_gather(block, axis, axis=0, tiled=True)
    groups = [list(range(k, n, 2)) for k in range(2)]
    mine = lax.all_gather(block, axis, axis_index_groups=groups)
    both = _pair(mine, _swap(mine, axis, 1), lax.axis_index(axis) % 2)
    return jnp.swapaxes(both, 0, 1).reshape(n * block.shape[0], block.shape[1])


def col_reduce_scatter(partial, axis="col"):
    n = lax.axis_size(axis)
    if n % 2:
        return lax.psum_scatter(partial, axis, scatter_dimension=0, tiled=True)
    m = partial.shape[0] // n
    k = lax.axis_index(axis) % 2
    by_core = jnp.swapaxes(partial.reshape(n // 2, 2, m, partial.shape[1]), 0, 1)
    chip = _pick(k, by_core) + _swap(_pick(1 - k, by_core), axis, 1)
    chips = n // 2
    z = lax.axis_index(axis) // 2
    if chips & (chips - 1):
        total = _pick(z, chip)
        for d in range(1, chips):
            pairs = [(2 * i + j, 2 * ((i + d) % chips) + j) for i in range(chips) for j in range(2)]
            total = total + lax.ppermute(_pick((z + d) % chips, chip), axis, pairs)
        return total
    levels = chips.bit_length() - 1
    cur = chip.reshape([2] * levels + [m, partial.shape[1]])
    bits = list(range(levels))[::-1]
    for bit in range(levels):
        mine = (z >> bit) & 1
        t = jnp.moveaxis(cur, bits.index(bit), 0)
        sent = _swap(_pick(1 - mine, t).astype(jnp.bfloat16), axis, 2 << bit)
        cur = _pick(mine, t) + sent.astype(jnp.float32)
        bits.remove(bit)
    return cur.reshape(m, partial.shape[1])


def body(tokens, weight, bias, cotangent):
    local_x = col_all_gather(tokens)
    my_rows = local_x.shape[0] // lax.axis_size("row")
    first_row = lax.axis_index("row") * my_rows
    partial_value = jnp.dot(local_x, weight, preferred_element_type=jnp.float32)
    preact = row_reduce_scatter(partial_value) + bias
    my_cot = lax.dynamic_slice_in_dim(cotangent, first_row, my_rows, 0)
    hidden, my_grad = activate(preact, my_cot)
    full_grad = row_all_gather(my_grad)
    grad_tokens = col_reduce_scatter(
        lax.dot_general(
            full_grad, weight, (((1,), (1,)), ((), ())), preferred_element_type=jnp.float32
        )
    ).astype(jnp.bfloat16)
    grad_weight = outer_product_sum(local_x.T, full_grad)
    grad_bias = jnp.sum(full_grad.astype(jnp.float32), axis=0)
    return (hidden, grad_tokens, grad_weight, grad_bias)


def solution(mesh):
    placed = (P("col", "row"), P("row", "col"), P("col"), P(None, "col"))
    return jax.shard_map(
        body,
        mesh=mesh,
        in_specs=placed,
        out_specs=(P("row", "col"), P("col", "row"), P("row", "col"), P("col")),
        check_vma=False,
    )
```

```python
import math

import jax
import jax.numpy as jnp
from jax import lax
from jax.experimental import pallas as pl
from jax.experimental.pallas import tpu as pltpu
from jax.sharding import PartitionSpec as P


def activate(preact, cotangent):
    normal_cdf = 0.5 * (1.0 + jax.scipy.special.erf(preact / math.sqrt(2.0)))
    normal_pdf = jnp.exp(-0.5 * preact * preact) / math.sqrt(2.0 * math.pi)
    hidden = (preact * normal_cdf).astype(jnp.bfloat16)
    grad_pre = (cotangent.astype(jnp.float32) * (normal_cdf + preact * normal_pdf)).astype(
        jnp.bfloat16
    )
    return (hidden, grad_pre)


def _outer_kernel(xt_ref, g_ref, o_ref):
    o_ref[...] = jnp.dot(xt_ref[...], g_ref[...], preferred_element_type=jnp.float32).astype(
        o_ref.dtype
    )


def outer_product_sum(xt, g, block_m=768, block_n=3072):
    m, k = xt.shape
    n = g.shape[1]
    block_m = min(block_m, m)
    block_n = min(block_n, n)
    return pl.pallas_call(
        _outer_kernel,
        grid=(n // block_n, m // block_m),
        in_specs=[
            pl.BlockSpec((block_m, k), lambda j, i: (i, 0)),
            pl.BlockSpec((k, block_n), lambda j, i: (0, j)),
        ],
        out_specs=pl.BlockSpec((block_m, block_n), lambda j, i: (i, j)),
        out_shape=jax.ShapeDtypeStruct((m, n), jnp.bfloat16),
        cost_estimate=pl.CostEstimate(
            flops=2 * m * n * k, transcendentals=0, bytes_accessed=2 * (m * k + k * n + m * n)
        ),
    )(xt, g)


def _swap(value, axis, flip):
    size = lax.axis_size(axis)
    return lax.ppermute(value, axis, [(i, i ^ flip) for i in range(size)])


def _pick(index, blocks):
    return lax.dynamic_index_in_dim(blocks, index, axis=0, keepdims=False)


def _halves(value):
    cols = value.shape[1]
    if cols % 256:
        return [value]
    return [value[:, : cols // 2], value[:, cols // 2 :]]


def _bit_orders(n):
    order = list(range(n.bit_length() - 1))
    return [order, order[::-1]]


def row_reduce_scatter(partial, axis="row"):
    n = lax.axis_size(axis)
    if n & (n - 1):
        return lax.psum_scatter(partial, axis, scatter_dimension=0, tiled=True)
    levels = n.bit_length() - 1
    r = lax.axis_index(axis)
    m = partial.shape[0] // n
    outs = []
    for half, order in zip(_halves(partial), _bit_orders(n)):
        cur = half.reshape([2] * levels + [m, half.shape[1]])
        bits = list(range(levels))[::-1]
        for bit in order:
            mine = (r >> bit) & 1
            t = jnp.moveaxis(cur, bits.index(bit), 0)
            sent = _swap(_pick(1 - mine, t).astype(jnp.bfloat16), axis, 1 << bit)
            cur = _pick(mine, t) + sent.astype(jnp.float32)
            bits.remove(bit)
        outs.append(cur.reshape(m, half.shape[1]))
    return jnp.concatenate(outs, axis=1)


def _pair(mine, theirs, bit):
    first = jnp.where(bit == 0, mine, theirs)
    second = jnp.where(bit == 0, theirs, mine)
    return jnp.stack([first, second], axis=0)


def row_all_gather(block, axis="row"):
    n = lax.axis_size(axis)
    if n & (n - 1):
        return lax.all_gather(block, axis, axis=0, tiled=True)
    levels = n.bit_length() - 1
    r = lax.axis_index(axis)
    m = block.shape[0]
    outs = []
    for half, order in zip(_halves(block), _bit_orders(n)):
        cur = half
        bits = []
        for bit in order:
            cur = _pair(cur, _swap(cur, axis, 1 << bit), (r >> bit) & 1)
            bits.insert(0, bit)
        perm = sorted(range(levels), key=lambda j: -bits[j])
        cur = jnp.transpose(cur, perm + [levels, levels + 1])
        outs.append(cur.reshape(n * m, half.shape[1]))
    return jnp.concatenate(outs, axis=1)


def col_all_gather(block, axis="col"):
    n = lax.axis_size(axis)
    if n % 2:
        return lax.all_gather(block, axis, axis=0, tiled=True)
    groups = [list(range(k, n, 2)) for k in range(2)]
    mine = lax.all_gather(block, axis, axis_index_groups=groups)
    both = _pair(mine, _swap(mine, axis, 1), lax.axis_index(axis) % 2)
    return jnp.swapaxes(both, 0, 1).reshape(n * block.shape[0], block.shape[1])


def col_reduce_scatter(rows_of, axis="col"):
    n = lax.axis_size(axis)
    k = lax.axis_index(axis) % 2
    sent = rows_of(1 - k)
    m = sent.shape[0] * 2 // n
    kept = lax.optimization_barrier(rows_of(k))
    chip = (kept + _swap(sent, axis, 1)).reshape(n // 2, m, sent.shape[1])
    chips = n // 2
    z = lax.axis_index(axis) // 2
    if chips & (chips - 1):
        total = _pick(z, chip)
        for d in range(1, chips):
            pairs = [(2 * i + j, 2 * ((i + d) % chips) + j) for i in range(chips) for j in range(2)]
            total = total + lax.ppermute(_pick((z + d) % chips, chip), axis, pairs)
        return total
    levels = chips.bit_length() - 1
    cur = chip.reshape([2] * levels + [m, sent.shape[1]])
    bits = list(range(levels))[::-1]
    for bit in range(levels):
        mine = (z >> bit) & 1
        t = jnp.moveaxis(cur, bits.index(bit), 0)
        moved = _swap(_pick(1 - mine, t).astype(jnp.bfloat16), axis, 2 << bit)
        cur = _pick(mine, t) + moved.astype(jnp.float32)
        bits.remove(bit)
    return cur.reshape(m, sent.shape[1])


def body(tokens, weight, bias, cotangent):
    local_x = col_all_gather(tokens)
    my_rows = local_x.shape[0] // lax.axis_size("row")
    first_row = lax.axis_index("row") * my_rows
    partial_value = jnp.dot(local_x, weight, preferred_element_type=jnp.float32)
    preact = row_reduce_scatter(partial_value) + bias
    my_cot = lax.dynamic_slice_in_dim(cotangent, first_row, my_rows, 0)
    hidden, my_grad = activate(preact, my_cot)
    full_grad = row_all_gather(my_grad)
    cols = lax.axis_size("col")
    if cols % 2:
        grad_tokens = lax.psum_scatter(
            lax.dot_general(
                full_grad, weight, (((1,), (1,)), ((), ())), preferred_element_type=jnp.float32
            ),
            "col",
            scatter_dimension=0,
            tiled=True,
        )
    else:
        by_core = jnp.swapaxes(full_grad.reshape(cols // 2, 2, -1, full_grad.shape[1]), 0, 1)

        def rows_of(j):
            g = _pick(j, by_core).reshape(-1, full_grad.shape[1])
            return lax.dot_general(
                g, weight, (((1,), (1,)), ((), ())), preferred_element_type=jnp.float32
            )

        grad_tokens = col_reduce_scatter(rows_of)
    grad_tokens = grad_tokens.astype(jnp.bfloat16)
    grad_weight = outer_product_sum(local_x.T, full_grad)
    grad_bias = jnp.sum(full_grad.astype(jnp.float32), axis=0)
    return (hidden, grad_tokens, grad_weight, grad_bias)


def solution(mesh):
    placed = (P("col", "row"), P("row", "col"), P("col"), P(None, "col"))
    return jax.shard_map(
        body,
        mesh=mesh,
        in_specs=placed,
        out_specs=(P("row", "col"), P("col", "row"), P("row", "col"), P("col")),
        check_vma=False,
    )
```

```python
import math

import jax
import jax.numpy as jnp
from jax import lax
from jax.experimental import pallas as pl
from jax.experimental.pallas import tpu as pltpu
from jax.sharding import PartitionSpec as P


def activate(preact, cotangent):
    normal_cdf = 0.5 * (1.0 + jax.scipy.special.erf(preact / math.sqrt(2.0)))
    normal_pdf = jnp.exp(-0.5 * preact * preact) / math.sqrt(2.0 * math.pi)
    hidden = (preact * normal_cdf).astype(jnp.bfloat16)
    grad_pre = (cotangent.astype(jnp.float32) * (normal_cdf + preact * normal_pdf)).astype(
        jnp.bfloat16
    )
    return (hidden, grad_pre)


def _outer_kernel(xt_ref, g_ref, o_ref):
    o_ref[...] = jnp.dot(xt_ref[...], g_ref[...], preferred_element_type=jnp.float32).astype(
        o_ref.dtype
    )


def outer_product_sum(xt, g, block_m=768, block_n=3072):
    m, k = xt.shape
    n = g.shape[1]
    block_m = min(block_m, m)
    block_n = min(block_n, n)
    return pl.pallas_call(
        _outer_kernel,
        grid=(n // block_n, m // block_m),
        in_specs=[
            pl.BlockSpec((block_m, k), lambda j, i: (i, 0)),
            pl.BlockSpec((k, block_n), lambda j, i: (0, j)),
        ],
        out_specs=pl.BlockSpec((block_m, block_n), lambda j, i: (i, j)),
        out_shape=jax.ShapeDtypeStruct((m, n), jnp.bfloat16),
        cost_estimate=pl.CostEstimate(
            flops=2 * m * n * k, transcendentals=0, bytes_accessed=2 * (m * k + k * n + m * n)
        ),
    )(xt, g)


def _swap(value, axis, flip):
    size = lax.axis_size(axis)
    return lax.ppermute(value, axis, [(i, i ^ flip) for i in range(size)])


def _pick(index, blocks):
    return lax.dynamic_index_in_dim(blocks, index, axis=0, keepdims=False)


def _halves(value):
    cols = value.shape[1]
    if cols % 256:
        return [value]
    return [value[:, : cols // 2], value[:, cols // 2 :]]


def _bit_orders(n):
    order = list(range(n.bit_length() - 1))
    return [order, order[::-1]]


def row_reduce_scatter(partial, axis="row"):
    n = lax.axis_size(axis)
    if n & (n - 1):
        return lax.psum_scatter(partial, axis, scatter_dimension=0, tiled=True)
    levels = n.bit_length() - 1
    r = lax.axis_index(axis)
    m = partial.shape[0] // n
    outs = []
    for half, order in zip(_halves(partial), _bit_orders(n)):
        cur = half.reshape([2] * levels + [m, half.shape[1]])
        bits = list(range(levels))[::-1]
        for bit in order:
            mine = (r >> bit) & 1
            t = jnp.moveaxis(cur, bits.index(bit), 0)
            sent = _swap(_pick(1 - mine, t).astype(jnp.bfloat16), axis, 1 << bit)
            cur = _pick(mine, t) + sent.astype(jnp.float32)
            bits.remove(bit)
        outs.append(cur.reshape(m, half.shape[1]))
    return jnp.concatenate(outs, axis=1)


def _pair(mine, theirs, bit):
    first = jnp.where(bit == 0, mine, theirs)
    second = jnp.where(bit == 0, theirs, mine)
    return jnp.stack([first, second], axis=0)


def row_all_gather(block, axis="row"):
    n = lax.axis_size(axis)
    if n & (n - 1):
        return lax.all_gather(block, axis, axis=0, tiled=True)
    levels = n.bit_length() - 1
    r = lax.axis_index(axis)
    m = block.shape[0]
    outs = []
    for half, order in zip(_halves(block), _bit_orders(n)):
        cur = half
        bits = []
        for bit in order:
            cur = _pair(cur, _swap(cur, axis, 1 << bit), (r >> bit) & 1)
            bits.insert(0, bit)
        perm = sorted(range(levels), key=lambda j: -bits[j])
        cur = jnp.transpose(cur, perm + [levels, levels + 1])
        outs.append(cur.reshape(n * m, half.shape[1]))
    return jnp.concatenate(outs, axis=1)


def col_all_gather(block, axis="col"):
    n = lax.axis_size(axis)
    if n % 2:
        return lax.all_gather(block, axis, axis=0, tiled=True)
    groups = [list(range(k, n, 2)) for k in range(2)]
    mine = lax.all_gather(block, axis, axis_index_groups=groups)
    both = _pair(mine, _swap(mine, axis, 1), lax.axis_index(axis) % 2)
    return jnp.swapaxes(both, 0, 1).reshape(n * block.shape[0], block.shape[1])


def col_reduce_scatter(partial, axis="col"):
    n = lax.axis_size(axis)
    if n % 2:
        return lax.psum_scatter(partial, axis, scatter_dimension=0, tiled=True)
    m = partial.shape[0] // n
    k = lax.axis_index(axis) % 2
    by_core = jnp.swapaxes(partial.reshape(n // 2, 2, m, partial.shape[1]), 0, 1)
    chip = _pick(k, by_core) + _swap(_pick(1 - k, by_core), axis, 1)
    chips = n // 2
    z = lax.axis_index(axis) // 2
    if chips & (chips - 1):
        total = _pick(z, chip)
        for d in range(1, chips):
            pairs = [(2 * i + j, 2 * ((i + d) % chips) + j) for i in range(chips) for j in range(2)]
            total = total + lax.ppermute(_pick((z + d) % chips, chip), axis, pairs)
        return total
    levels = chips.bit_length() - 1
    cur = chip.reshape([2] * levels + [m, partial.shape[1]])
    bits = list(range(levels))[::-1]
    for bit in range(levels):
        mine = (z >> bit) & 1
        t = jnp.moveaxis(cur, bits.index(bit), 0)
        sent = _swap(_pick(1 - mine, t).astype(jnp.bfloat16), axis, 2 << bit)
        cur = _pick(mine, t) + sent.astype(jnp.float32)
        bits.remove(bit)
    return cur.reshape(m, partial.shape[1])


def _block(size, preferred):
    for b in (preferred, 256, 128):
        if size % b == 0:
            return min(b, size)
    return size


def _mm_kernel(x_ref, w_ref, o_ref):
    o_ref[...] = jnp.dot(x_ref[...], w_ref[...], preferred_element_type=jnp.float32)


def matmul(x, w):
    m, k = x.shape
    n = w.shape[1]
    bn = _block(n, 512)
    return pl.pallas_call(
        _mm_kernel,
        grid=(n // bn,),
        in_specs=[
            pl.BlockSpec((m, k), lambda j: (0, 0)),
            pl.BlockSpec((k, bn), lambda j: (0, j)),
        ],
        out_specs=pl.BlockSpec((m, bn), lambda j: (0, j)),
        out_shape=jax.ShapeDtypeStruct((m, n), jnp.float32),
        cost_estimate=pl.CostEstimate(
            flops=2 * m * n * k, transcendentals=0, bytes_accessed=2 * (m * k + k * n) + 4 * m * n
        ),
    )(x, w)


def _mm_nt_kernel(g_ref, w_ref, o_ref):
    o_ref[...] = lax.dot_general(
        g_ref[...], w_ref[...], (((1,), (1,)), ((), ())), preferred_element_type=jnp.float32
    )


def matmul_nt(g, w):
    m, k = g.shape
    n = w.shape[0]
    bn = _block(n, 512)
    return pl.pallas_call(
        _mm_nt_kernel,
        grid=(n // bn,),
        in_specs=[
            pl.BlockSpec((m, k), lambda i: (0, 0)),
            pl.BlockSpec((bn, k), lambda i: (i, 0)),
        ],
        out_specs=pl.BlockSpec((m, bn), lambda i: (0, i)),
        out_shape=jax.ShapeDtypeStruct((m, n), jnp.float32),
        cost_estimate=pl.CostEstimate(
            flops=2 * m * n * k, transcendentals=0, bytes_accessed=2 * (m * k + k * n) + 4 * m * n
        ),
    )(g, w)


def body(tokens, weight, bias, cotangent):
    local_x = col_all_gather(tokens)
    my_rows = local_x.shape[0] // lax.axis_size("row")
    first_row = lax.axis_index("row") * my_rows
    partial_value = matmul(local_x, weight)
    preact = row_reduce_scatter(partial_value) + bias
    my_cot = lax.dynamic_slice_in_dim(cotangent, first_row, my_rows, 0)
    hidden, my_grad = activate(preact, my_cot)
    full_grad = row_all_gather(my_grad)
    grad_tokens = col_reduce_scatter(
        matmul_nt(full_grad, weight)
    ).astype(jnp.bfloat16)
    grad_weight = outer_product_sum(local_x.T, full_grad)
    grad_bias = jnp.sum(full_grad.astype(jnp.float32), axis=0)
    return (hidden, grad_tokens, grad_weight, grad_bias)


def solution(mesh):
    placed = (P("col", "row"), P("row", "col"), P("col"), P(None, "col"))
    return jax.shard_map(
        body,
        mesh=mesh,
        in_specs=placed,
        out_specs=(P("row", "col"), P("col", "row"), P("row", "col"), P("col")),
        check_vma=False,
    )
```

```python
import math

import jax
import jax.numpy as jnp
from jax import lax
from jax.experimental import pallas as pl
from jax.experimental.pallas import tpu as pltpu
from jax.sharding import PartitionSpec as P


def activate(preact, cotangent):
    normal_cdf = 0.5 * (1.0 + jax.scipy.special.erf(preact / math.sqrt(2.0)))
    normal_pdf = jnp.exp(-0.5 * preact * preact) / math.sqrt(2.0 * math.pi)
    hidden = (preact * normal_cdf).astype(jnp.bfloat16)
    grad_pre = (cotangent.astype(jnp.float32) * (normal_cdf + preact * normal_pdf)).astype(
        jnp.bfloat16
    )
    return (hidden, grad_pre)


def _outer_kernel(xt_ref, g_ref, o_ref):
    o_ref[...] = jnp.dot(xt_ref[...], g_ref[...], preferred_element_type=jnp.float32).astype(
        o_ref.dtype
    )


def outer_product_sum(xt, g, block_m=768, block_n=3072):
    m, k = xt.shape
    n = g.shape[1]
    block_m = min(block_m, m)
    block_n = min(block_n, n)
    return pl.pallas_call(
        _outer_kernel,
        grid=(n // block_n, m // block_m),
        in_specs=[
            pl.BlockSpec((block_m, k), lambda j, i: (i, 0)),
            pl.BlockSpec((k, block_n), lambda j, i: (0, j)),
        ],
        out_specs=pl.BlockSpec((block_m, block_n), lambda j, i: (i, j)),
        out_shape=jax.ShapeDtypeStruct((m, n), jnp.bfloat16),
        cost_estimate=pl.CostEstimate(
            flops=2 * m * n * k, transcendentals=0, bytes_accessed=2 * (m * k + k * n + m * n)
        ),
    )(xt, g)


def _swap(value, axis, flip):
    size = lax.axis_size(axis)
    return lax.ppermute(value, axis, [(i, i ^ flip) for i in range(size)])


def _pick(index, blocks):
    return lax.dynamic_index_in_dim(blocks, index, axis=0, keepdims=False)


def _halves(value):
    cols = value.shape[1]
    if cols % 256:
        return [value]
    return [value[:, : cols // 2], value[:, cols // 2 :]]


def _bit_orders(n):
    order = list(range(n.bit_length() - 1))
    return [order, order[::-1]]


def row_reduce_scatter(partial, axis="row"):
    n = lax.axis_size(axis)
    if n & (n - 1):
        return lax.psum_scatter(partial, axis, scatter_dimension=0, tiled=True)
    levels = n.bit_length() - 1
    r = lax.axis_index(axis)
    m = partial.shape[0] // n
    outs = []
    for half, order in zip(_halves(partial), _bit_orders(n)):
        cur = half.reshape([2] * levels + [m, half.shape[1]])
        bits = list(range(levels))[::-1]
        for bit in order:
            mine = (r >> bit) & 1
            t = jnp.moveaxis(cur, bits.index(bit), 0)
            sent = _swap(_pick(1 - mine, t).astype(jnp.bfloat16), axis, 1 << bit)
            cur = _pick(mine, t) + sent.astype(jnp.float32)
            bits.remove(bit)
        outs.append(cur.reshape(m, half.shape[1]))
    return jnp.concatenate(outs, axis=1)


def _pair(mine, theirs, bit):
    first = jnp.where(bit == 0, mine, theirs)
    second = jnp.where(bit == 0, theirs, mine)
    return jnp.stack([first, second], axis=0)


def row_all_gather(block, axis="row"):
    n = lax.axis_size(axis)
    if n & (n - 1):
        return lax.all_gather(block, axis, axis=0, tiled=True)
    levels = n.bit_length() - 1
    r = lax.axis_index(axis)
    m = block.shape[0]
    outs = []
    for half, order in zip(_halves(block), _bit_orders(n)):
        cur = half
        bits = []
        for bit in order:
            cur = _pair(cur, _swap(cur, axis, 1 << bit), (r >> bit) & 1)
            bits.insert(0, bit)
        perm = sorted(range(levels), key=lambda j: -bits[j])
        cur = jnp.transpose(cur, perm + [levels, levels + 1])
        outs.append(cur.reshape(n * m, half.shape[1]))
    return jnp.concatenate(outs, axis=1)


def col_all_gather(block, axis="col"):
    n = lax.axis_size(axis)
    if n % 2:
        return lax.all_gather(block, axis, axis=0, tiled=True)
    groups = [list(range(k, n, 2)) for k in range(2)]
    mine = lax.all_gather(block, axis, axis_index_groups=groups)
    both = _pair(mine, _swap(mine, axis, 1), lax.axis_index(axis) % 2)
    return jnp.swapaxes(both, 0, 1).reshape(n * block.shape[0], block.shape[1])


def col_reduce_scatter(partial, axis="col"):
    n = lax.axis_size(axis)
    if n % 2:
        return lax.psum_scatter(partial, axis, scatter_dimension=0, tiled=True)
    m = partial.shape[0] // n
    k = lax.axis_index(axis) % 2
    by_core = jnp.swapaxes(partial.reshape(n // 2, 2, m, partial.shape[1]), 0, 1)
    moved = _swap(_pick(1 - k, by_core).astype(jnp.bfloat16), axis, 1)
    chip = _pick(k, by_core) + moved.astype(jnp.float32)
    chips = n // 2
    z = lax.axis_index(axis) // 2
    if chips & (chips - 1):
        total = _pick(z, chip)
        for d in range(1, chips):
            pairs = [(2 * i + j, 2 * ((i + d) % chips) + j) for i in range(chips) for j in range(2)]
            total = total + lax.ppermute(_pick((z + d) % chips, chip), axis, pairs)
        return total
    levels = chips.bit_length() - 1
    cur = chip.reshape([2] * levels + [m, partial.shape[1]])
    bits = list(range(levels))[::-1]
    for bit in range(levels):
        mine = (z >> bit) & 1
        t = jnp.moveaxis(cur, bits.index(bit), 0)
        sent = _swap(_pick(1 - mine, t).astype(jnp.bfloat16), axis, 2 << bit)
        cur = _pick(mine, t) + sent.astype(jnp.float32)
        bits.remove(bit)
    return cur.reshape(m, partial.shape[1])


def body(tokens, weight, bias, cotangent):
    local_x = col_all_gather(tokens)
    my_rows = local_x.shape[0] // lax.axis_size("row")
    first_row = lax.axis_index("row") * my_rows
    partial_value = jnp.dot(local_x, weight, preferred_element_type=jnp.float32)
    preact = row_reduce_scatter(partial_value) + bias
    my_cot = lax.dynamic_slice_in_dim(cotangent, first_row, my_rows, 0)
    hidden, my_grad = activate(preact, my_cot)
    full_grad = row_all_gather(my_grad)
    grad_tokens = col_reduce_scatter(
        lax.dot_general(
            full_grad, weight, (((1,), (1,)), ((), ())), preferred_element_type=jnp.float32
        )
    ).astype(jnp.bfloat16)
    grad_weight = outer_product_sum(local_x.T, full_grad)
    grad_bias = jnp.sum(full_grad.astype(jnp.float32), axis=0)
    return (hidden, grad_tokens, grad_weight, grad_bias)


def solution(mesh):
    placed = (P("col", "row"), P("row", "col"), P("col"), P(None, "col"))
    return jax.shard_map(
        body,
        mesh=mesh,
        in_specs=placed,
        out_specs=(P("row", "col"), P("col", "row"), P("row", "col"), P("col")),
        check_vma=False,
    )
```

```python
import math

import jax
import jax.numpy as jnp
from jax import lax
from jax.experimental import pallas as pl
from jax.experimental.pallas import tpu as pltpu
from jax.sharding import PartitionSpec as P


def activate(preact, cotangent):
    normal_cdf = 0.5 * (1.0 + jax.scipy.special.erf(preact / math.sqrt(2.0)))
    normal_pdf = jnp.exp(-0.5 * preact * preact) / math.sqrt(2.0 * math.pi)
    hidden = (preact * normal_cdf).astype(jnp.bfloat16)
    grad_pre = (cotangent.astype(jnp.float32) * (normal_cdf + preact * normal_pdf)).astype(
        jnp.bfloat16
    )
    return (hidden, grad_pre)


def _outer_kernel(xt_ref, g_ref, o_ref):
    o_ref[...] = jnp.dot(xt_ref[...], g_ref[...], preferred_element_type=jnp.float32).astype(
        o_ref.dtype
    )


def _outer_into_kernel(xt_ref, g_ref, _, o_ref):
    _outer_kernel(xt_ref, g_ref, o_ref)


def outer_product_sum(xt, g, first=0, count=None, into=None, block_m=768, block_n=3072):
    m, k = xt.shape
    n = g.shape[1]
    block_m = min(block_m, m)
    block_n = min(block_n, n)
    if count is None:
        count = m // block_m - first
    in_specs = [
        pl.BlockSpec((block_m, k), lambda j, i: (i + first, 0)),
        pl.BlockSpec((k, block_n), lambda j, i: (0, j)),
    ]
    operands = [xt, g]
    kernel, aliases = _outer_kernel, {}
    if into is not None:
        in_specs.append(pl.BlockSpec(memory_space=pl.ANY))
        operands.append(into)
        kernel, aliases = _outer_into_kernel, {2: 0}
    rows = count * block_m
    return pl.pallas_call(
        kernel,
        grid=(n // block_n, count),
        in_specs=in_specs,
        out_specs=pl.BlockSpec((block_m, block_n), lambda j, i: (i + first, j)),
        out_shape=jax.ShapeDtypeStruct((m, n), jnp.bfloat16),
        input_output_aliases=aliases,
        cost_estimate=pl.CostEstimate(
            flops=2 * rows * n * k, transcendentals=0, bytes_accessed=2 * (rows * k + k * n + rows * n)
        ),
    )(*operands)


def _swap(value, axis, flip):
    size = lax.axis_size(axis)
    return lax.ppermute(value, axis, [(i, i ^ flip) for i in range(size)])


def _pick(index, blocks):
    return lax.dynamic_index_in_dim(blocks, index, axis=0, keepdims=False)


def _halves(value):
    cols = value.shape[1]
    if cols % 256:
        return [value]
    return [value[:, : cols // 2], value[:, cols // 2 :]]


def _bit_orders(n):
    order = list(range(n.bit_length() - 1))
    return [order, order[::-1]]


def row_reduce_scatter(partial, axis="row"):
    n = lax.axis_size(axis)
    if n & (n - 1):
        return lax.psum_scatter(partial, axis, scatter_dimension=0, tiled=True)
    levels = n.bit_length() - 1
    r = lax.axis_index(axis)
    m = partial.shape[0] // n
    outs = []
    for half, order in zip(_halves(partial), _bit_orders(n)):
        cur = half.reshape([2] * levels + [m, half.shape[1]])
        bits = list(range(levels))[::-1]
        for bit in order:
            mine = (r >> bit) & 1
            t = jnp.moveaxis(cur, bits.index(bit), 0)
            sent = _swap(_pick(1 - mine, t).astype(jnp.bfloat16), axis, 1 << bit)
            cur = _pick(mine, t) + sent.astype(jnp.float32)
            bits.remove(bit)
        outs.append(cur.reshape(m, half.shape[1]))
    return jnp.concatenate(outs, axis=1)


def _pair(mine, theirs, bit):
    first = jnp.where(bit == 0, mine, theirs)
    second = jnp.where(bit == 0, theirs, mine)
    return jnp.stack([first, second], axis=0)


def row_all_gather(block, axis="row"):
    n = lax.axis_size(axis)
    if n & (n - 1):
        return lax.all_gather(block, axis, axis=0, tiled=True)
    levels = n.bit_length() - 1
    r = lax.axis_index(axis)
    m = block.shape[0]
    outs = []
    for half, order in zip(_halves(block), _bit_orders(n)):
        cur = half
        bits = []
        for bit in order:
            cur = _pair(cur, _swap(cur, axis, 1 << bit), (r >> bit) & 1)
            bits.insert(0, bit)
        perm = sorted(range(levels), key=lambda j: -bits[j])
        cur = jnp.transpose(cur, perm + [levels, levels + 1])
        outs.append(cur.reshape(n * m, half.shape[1]))
    return jnp.concatenate(outs, axis=1)


def col_all_gather(block, axis="col"):
    n = lax.axis_size(axis)
    if n % 2:
        return lax.all_gather(block, axis, axis=0, tiled=True)
    groups = [list(range(k, n, 2)) for k in range(2)]
    mine = lax.all_gather(block, axis, axis_index_groups=groups)
    both = _pair(mine, _swap(mine, axis, 1), lax.axis_index(axis) % 2)
    return jnp.swapaxes(both, 0, 1).reshape(n * block.shape[0], block.shape[1])


def col_reduce_scatter(partial, hold, axis="col"):
    n = lax.axis_size(axis)
    if n % 2:
        return lax.psum_scatter(partial, axis, scatter_dimension=0, tiled=True), hold
    m = partial.shape[0] // n
    k = lax.axis_index(axis) % 2
    by_core = jnp.swapaxes(partial.reshape(n // 2, 2, m, partial.shape[1]), 0, 1)
    chip = _pick(k, by_core) + _swap(_pick(1 - k, by_core), axis, 1)
    chips = n // 2
    z = lax.axis_index(axis) // 2
    if chips & (chips - 1):
        total = _pick(z, chip)
        for d in range(1, chips):
            pairs = [(2 * i + j, 2 * ((i + d) % chips) + j) for i in range(chips) for j in range(2)]
            total = total + lax.ppermute(_pick((z + d) % chips, chip), axis, pairs)
        return total, hold
    levels = chips.bit_length() - 1
    cur = chip.reshape([2] * levels + [m, partial.shape[1]])
    bits = list(range(levels))[::-1]
    for bit in range(levels):
        mine = (z >> bit) & 1
        t = jnp.moveaxis(cur, bits.index(bit), 0)
        sent = _swap(_pick(1 - mine, t).astype(jnp.bfloat16), axis, 2 << bit)
        cur = _pick(mine, t) + sent.astype(jnp.float32)
        bits.remove(bit)
        if bit == 0:
            cur, hold = lax.optimization_barrier((cur, hold))
    return cur.reshape(m, partial.shape[1]), hold


def body(tokens, weight, bias, cotangent):
    local_x = col_all_gather(tokens)
    my_rows = local_x.shape[0] // lax.axis_size("row")
    first_row = lax.axis_index("row") * my_rows
    partial_value = jnp.dot(local_x, weight, preferred_element_type=jnp.float32)
    preact = row_reduce_scatter(partial_value) + bias
    my_cot = lax.dynamic_slice_in_dim(cotangent, first_row, my_rows, 0)
    hidden, my_grad = activate(preact, my_cot)
    full_grad = row_all_gather(my_grad)
    local_xt = local_x.T
    blocks = local_xt.shape[0] // min(768, local_xt.shape[0])
    first_half = outer_product_sum(local_xt, full_grad, 0, blocks // 2)
    grad_tokens, first_half = col_reduce_scatter(
        lax.dot_general(
            full_grad, weight, (((1,), (1,)), ((), ())), preferred_element_type=jnp.float32
        ),
        first_half,
    )
    grad_tokens = grad_tokens.astype(jnp.bfloat16)
    if blocks // 2:
        grad_weight = outer_product_sum(local_xt, full_grad, blocks // 2, into=first_half)
    else:
        grad_weight = outer_product_sum(local_xt, full_grad)
    grad_bias = jnp.sum(full_grad.astype(jnp.float32), axis=0)
    return (hidden, grad_tokens, grad_weight, grad_bias)


def solution(mesh):
    placed = (P("col", "row"), P("row", "col"), P("col"), P(None, "col"))
    return jax.shard_map(
        body,
        mesh=mesh,
        in_specs=placed,
        out_specs=(P("row", "col"), P("col", "row"), P("row", "col"), P("col")),
        check_vma=False,
    )
```

```python
import math

import jax
import jax.numpy as jnp
from jax import lax
from jax.experimental import pallas as pl
from jax.experimental.pallas import tpu as pltpu
from jax.sharding import PartitionSpec as P


def activate(preact, cotangent):
    normal_cdf = 0.5 * (1.0 + jax.scipy.special.erf(preact / math.sqrt(2.0)))
    normal_pdf = jnp.exp(-0.5 * preact * preact) / math.sqrt(2.0 * math.pi)
    hidden = (preact * normal_cdf).astype(jnp.bfloat16)
    grad_pre = (cotangent.astype(jnp.float32) * (normal_cdf + preact * normal_pdf)).astype(
        jnp.bfloat16
    )
    return (hidden, grad_pre)


def _outer_kernel(xt_ref, g_ref, o_ref):
    o_ref[...] = jnp.dot(xt_ref[...], g_ref[...], preferred_element_type=jnp.float32).astype(
        o_ref.dtype
    )


def _outer_into_kernel(xt_ref, g_ref, _, o_ref):
    _outer_kernel(xt_ref, g_ref, o_ref)


def outer_product_sum(xt, g, first=0, count=None, into=None, block_m=768, block_n=3072):
    m, k = xt.shape
    n = g.shape[1]
    block_m = min(block_m, m)
    block_n = min(block_n, n)
    if count is None:
        count = m // block_m - first
    in_specs = [
        pl.BlockSpec((block_m, k), lambda j, i: (i + first, 0)),
        pl.BlockSpec((k, block_n), lambda j, i: (0, j)),
    ]
    operands = [xt, g]
    kernel, aliases = _outer_kernel, {}
    if into is not None:
        in_specs.append(pl.BlockSpec(memory_space=pl.ANY))
        operands.append(into)
        kernel, aliases = _outer_into_kernel, {2: 0}
    rows = count * block_m
    return pl.pallas_call(
        kernel,
        grid=(n // block_n, count),
        in_specs=in_specs,
        out_specs=pl.BlockSpec((block_m, block_n), lambda j, i: (i + first, j)),
        out_shape=jax.ShapeDtypeStruct((m, n), jnp.bfloat16),
        input_output_aliases=aliases,
        cost_estimate=pl.CostEstimate(
            flops=2 * rows * n * k, transcendentals=0, bytes_accessed=2 * (rows * k + k * n + rows * n)
        ),
    )(*operands)


def _swap(value, axis, flip):
    size = lax.axis_size(axis)
    return lax.ppermute(value, axis, [(i, i ^ flip) for i in range(size)])


def _pick(index, blocks):
    return lax.dynamic_index_in_dim(blocks, index, axis=0, keepdims=False)


def _halves(value):
    cols = value.shape[1]
    if cols % 256:
        return [value]
    return [value[:, : cols // 2], value[:, cols // 2 :]]


def _bit_orders(n):
    order = list(range(n.bit_length() - 1))
    return [order, order[::-1]]


def row_reduce_scatter(partial, axis="row"):
    n = lax.axis_size(axis)
    if n & (n - 1):
        return lax.psum_scatter(partial, axis, scatter_dimension=0, tiled=True)
    levels = n.bit_length() - 1
    r = lax.axis_index(axis)
    m = partial.shape[0] // n
    outs = []
    for half, order in zip(_halves(partial), _bit_orders(n)):
        cur = half.reshape([2] * levels + [m, half.shape[1]])
        bits = list(range(levels))[::-1]
        for bit in order:
            mine = (r >> bit) & 1
            t = jnp.moveaxis(cur, bits.index(bit), 0)
            sent = _swap(_pick(1 - mine, t).astype(jnp.bfloat16), axis, 1 << bit)
            cur = _pick(mine, t) + sent.astype(jnp.float32)
            bits.remove(bit)
        outs.append(cur.reshape(m, half.shape[1]))
    return jnp.concatenate(outs, axis=1)


def _pair(mine, theirs, bit):
    first = jnp.where(bit == 0, mine, theirs)
    second = jnp.where(bit == 0, theirs, mine)
    return jnp.stack([first, second], axis=0)


def row_all_gather(block, axis="row"):
    n = lax.axis_size(axis)
    if n & (n - 1):
        return lax.all_gather(block, axis, axis=0, tiled=True)
    levels = n.bit_length() - 1
    r = lax.axis_index(axis)
    m = block.shape[0]
    outs = []
    for half, order in zip(_halves(block), _bit_orders(n)):
        cur = half
        bits = []
        for bit in order:
            cur = _pair(cur, _swap(cur, axis, 1 << bit), (r >> bit) & 1)
            bits.insert(0, bit)
        perm = sorted(range(levels), key=lambda j: -bits[j])
        cur = jnp.transpose(cur, perm + [levels, levels + 1])
        outs.append(cur.reshape(n * m, half.shape[1]))
    return jnp.concatenate(outs, axis=1)


def col_all_gather(block, axis="col"):
    n = lax.axis_size(axis)
    if n % 2:
        return lax.all_gather(block, axis, axis=0, tiled=True)
    groups = [list(range(k, n, 2)) for k in range(2)]
    mine = lax.all_gather(block, axis, axis_index_groups=groups)
    both = _pair(mine, _swap(mine, axis, 1), lax.axis_index(axis) % 2)
    return jnp.swapaxes(both, 0, 1).reshape(n * block.shape[0], block.shape[1])


def col_reduce_scatter(partial, hold, axis="col"):
    n = lax.axis_size(axis)
    if n % 2:
        return lax.psum_scatter(partial, axis, scatter_dimension=0, tiled=True), hold
    m = partial.shape[0] // n
    k = lax.axis_index(axis) % 2
    by_core = jnp.swapaxes(partial.reshape(n // 2, 2, m, partial.shape[1]), 0, 1)
    moved = _swap(_pick(1 - k, by_core).astype(jnp.bfloat16), axis, 1)
    chip = _pick(k, by_core) + moved.astype(jnp.float32)
    chips = n // 2
    z = lax.axis_index(axis) // 2
    if chips & (chips - 1):
        total = _pick(z, chip)
        for d in range(1, chips):
            pairs = [(2 * i + j, 2 * ((i + d) % chips) + j) for i in range(chips) for j in range(2)]
            total = total + lax.ppermute(_pick((z + d) % chips, chip), axis, pairs)
        return total, hold
    levels = chips.bit_length() - 1
    cur = chip.reshape([2] * levels + [m, partial.shape[1]])
    bits = list(range(levels))[::-1]
    for bit in range(levels):
        mine = (z >> bit) & 1
        t = jnp.moveaxis(cur, bits.index(bit), 0)
        sent = _swap(_pick(1 - mine, t).astype(jnp.bfloat16), axis, 2 << bit)
        cur = _pick(mine, t) + sent.astype(jnp.float32)
        bits.remove(bit)
        if bit == 0:
            cur, hold = lax.optimization_barrier((cur, hold))
    return cur.reshape(m, partial.shape[1]), hold


def body(tokens, weight, bias, cotangent):
    local_x = col_all_gather(tokens)
    my_rows = local_x.shape[0] // lax.axis_size("row")
    first_row = lax.axis_index("row") * my_rows
    partial_value = jnp.dot(local_x, weight, preferred_element_type=jnp.float32)
    preact = row_reduce_scatter(partial_value) + bias
    my_cot = lax.dynamic_slice_in_dim(cotangent, first_row, my_rows, 0)
    hidden, my_grad = activate(preact, my_cot)
    full_grad = row_all_gather(my_grad)
    local_xt = local_x.T
    blocks = local_xt.shape[0] // min(768, local_xt.shape[0])
    first_half = outer_product_sum(local_xt, full_grad, 0, blocks // 2)
    grad_tokens, first_half = col_reduce_scatter(
        lax.dot_general(
            full_grad, weight, (((1,), (1,)), ((), ())), preferred_element_type=jnp.float32
        ),
        first_half,
    )
    grad_tokens = grad_tokens.astype(jnp.bfloat16)
    if blocks // 2:
        grad_weight = outer_product_sum(local_xt, full_grad, blocks // 2, into=first_half)
    else:
        grad_weight = outer_product_sum(local_xt, full_grad)
    grad_bias = jnp.sum(full_grad.astype(jnp.float32), axis=0)
    return (hidden, grad_tokens, grad_weight, grad_bias)


def solution(mesh):
    placed = (P("col", "row"), P("row", "col"), P("col"), P(None, "col"))
    return jax.shard_map(
        body,
        mesh=mesh,
        in_specs=placed,
        out_specs=(P("row", "col"), P("col", "row"), P("row", "col"), P("col")),
        check_vma=False,
    )
```

```python
import math

import jax
import jax.numpy as jnp
from jax import lax
from jax.experimental import pallas as pl
from jax.experimental.pallas import tpu as pltpu
from jax.sharding import PartitionSpec as P


def activate(preact, cotangent):
    normal_cdf = 0.5 * (1.0 + jax.scipy.special.erf(preact / math.sqrt(2.0)))
    normal_pdf = jnp.exp(-0.5 * preact * preact) / math.sqrt(2.0 * math.pi)
    hidden = (preact * normal_cdf).astype(jnp.bfloat16)
    grad_pre = (cotangent.astype(jnp.float32) * (normal_cdf + preact * normal_pdf)).astype(
        jnp.bfloat16
    )
    return (hidden, grad_pre)


def _outer_kernel(xt_ref, g_ref, o_ref):
    o_ref[...] = jnp.dot(xt_ref[...], g_ref[...], preferred_element_type=jnp.float32).astype(
        o_ref.dtype
    )


def _outer_into_kernel(xt_ref, g_ref, _, o_ref):
    _outer_kernel(xt_ref, g_ref, o_ref)


def outer_product_sum(xt, g, first=0, count=None, into=None, block_m=768, block_n=3072):
    m, k = xt.shape
    n = g.shape[1]
    block_m = min(block_m, m)
    block_n = min(block_n, n)
    if count is None:
        count = m // block_m - first
    in_specs = [
        pl.BlockSpec((block_m, k), lambda j, i: (i + first, 0)),
        pl.BlockSpec((k, block_n), lambda j, i: (0, j)),
    ]
    operands = [xt, g]
    kernel, aliases = _outer_kernel, {}
    if into is not None:
        in_specs.append(pl.BlockSpec(memory_space=pl.ANY))
        operands.append(into)
        kernel, aliases = _outer_into_kernel, {2: 0}
    rows = count * block_m
    return pl.pallas_call(
        kernel,
        grid=(n // block_n, count),
        in_specs=in_specs,
        out_specs=pl.BlockSpec((block_m, block_n), lambda j, i: (i + first, j)),
        out_shape=jax.ShapeDtypeStruct((m, n), jnp.bfloat16),
        input_output_aliases=aliases,
        cost_estimate=pl.CostEstimate(
            flops=2 * rows * n * k, transcendentals=0, bytes_accessed=2 * (rows * k + k * n + rows * n)
        ),
    )(*operands)


def _swap(value, axis, flip):
    size = lax.axis_size(axis)
    return lax.ppermute(value, axis, [(i, i ^ flip) for i in range(size)])


def _pick(index, blocks):
    return lax.dynamic_index_in_dim(blocks, index, axis=0, keepdims=False)


def _halves(value):
    cols = value.shape[1]
    if cols % 256:
        return [value]
    return [value[:, : cols // 2], value[:, cols // 2 :]]


def _bit_orders(n):
    order = list(range(n.bit_length() - 1))
    return [order, order[::-1]]


def row_reduce_scatter(partial, axis="row"):
    n = lax.axis_size(axis)
    if n & (n - 1):
        return lax.psum_scatter(partial, axis, scatter_dimension=0, tiled=True)
    levels = n.bit_length() - 1
    r = lax.axis_index(axis)
    m = partial.shape[0] // n
    outs = []
    for half, order in zip(_halves(partial), _bit_orders(n)):
        cur = half.reshape([2] * levels + [m, half.shape[1]])
        bits = list(range(levels))[::-1]
        for bit in order:
            mine = (r >> bit) & 1
            t = jnp.moveaxis(cur, bits.index(bit), 0)
            sent = _swap(_pick(1 - mine, t).astype(jnp.bfloat16), axis, 1 << bit)
            cur = _pick(mine, t) + sent.astype(jnp.float32)
            bits.remove(bit)
        outs.append(cur.reshape(m, half.shape[1]))
    return jnp.concatenate(outs, axis=1)


def _pair(mine, theirs, bit):
    first = jnp.where(bit == 0, mine, theirs)
    second = jnp.where(bit == 0, theirs, mine)
    return jnp.stack([first, second], axis=0)


def row_all_gather(block, axis="row"):
    n = lax.axis_size(axis)
    if n & (n - 1):
        return lax.all_gather(block, axis, axis=0, tiled=True)
    levels = n.bit_length() - 1
    r = lax.axis_index(axis)
    m = block.shape[0]
    outs = []
    for half, order in zip(_halves(block), _bit_orders(n)):
        cur = half
        bits = []
        for bit in order:
            cur = _pair(cur, _swap(cur, axis, 1 << bit), (r >> bit) & 1)
            bits.insert(0, bit)
        perm = sorted(range(levels), key=lambda j: -bits[j])
        cur = jnp.transpose(cur, perm + [levels, levels + 1])
        outs.append(cur.reshape(n * m, half.shape[1]))
    return jnp.concatenate(outs, axis=1)


def col_all_gather(block, axis="col"):
    n = lax.axis_size(axis)
    if n % 2:
        return lax.all_gather(block, axis, axis=0, tiled=True)
    groups = [list(range(k, n, 2)) for k in range(2)]
    mine = lax.all_gather(block, axis, axis_index_groups=groups)
    both = _pair(mine, _swap(mine, axis, 1), lax.axis_index(axis) % 2)
    return jnp.swapaxes(both, 0, 1).reshape(n * block.shape[0], block.shape[1])


def col_reduce_scatter(partial, hold, axis="col"):
    n = lax.axis_size(axis)
    if n % 2:
        return lax.psum_scatter(partial, axis, scatter_dimension=0, tiled=True), hold
    m = partial.shape[0] // n
    k = lax.axis_index(axis) % 2
    by_core = jnp.swapaxes(partial.reshape(n // 2, 2, m, partial.shape[1]), 0, 1)
    moved = _swap(_pick(1 - k, by_core).astype(jnp.bfloat16), axis, 1)
    chip = _pick(k, by_core) + moved.astype(jnp.float32)
    chips = n // 2
    z = lax.axis_index(axis) // 2
    if chips & (chips - 1):
        total = _pick(z, chip)
        for d in range(1, chips):
            pairs = [(2 * i + j, 2 * ((i + d) % chips) + j) for i in range(chips) for j in range(2)]
            total = total + lax.ppermute(_pick((z + d) % chips, chip), axis, pairs)
        return total, hold
    levels = chips.bit_length() - 1
    halves = _halves(chip.reshape(chips * m, -1))
    orders = _bit_orders(chips)
    outs = []
    for half, order in zip(halves, orders):
        cur = half.reshape([2] * levels + [m, half.shape[1]])
        bits = list(range(levels))[::-1]
        for bit in order:
            mine = (z >> bit) & 1
            t = jnp.moveaxis(cur, bits.index(bit), 0)
            sent = _swap(_pick(1 - mine, t).astype(jnp.bfloat16), axis, 2 << bit)
            cur = _pick(mine, t) + sent.astype(jnp.float32)
            bits.remove(bit)
            if len(bits) == levels - 1:
                cur, hold = lax.optimization_barrier((cur, hold))
        outs.append(cur.reshape(m, half.shape[1]))
    return jnp.concatenate(outs, axis=1), hold


def body(tokens, weight, bias, cotangent):
    local_x = col_all_gather(tokens)
    my_rows = local_x.shape[0] // lax.axis_size("row")
    first_row = lax.axis_index("row") * my_rows
    partial_value = jnp.dot(local_x, weight, preferred_element_type=jnp.float32)
    preact = row_reduce_scatter(partial_value) + bias
    my_cot = lax.dynamic_slice_in_dim(cotangent, first_row, my_rows, 0)
    hidden, my_grad = activate(preact, my_cot)
    full_grad = row_all_gather(my_grad)
    local_xt = local_x.T
    blocks = local_xt.shape[0] // min(768, local_xt.shape[0])
    first_half = outer_product_sum(local_xt, full_grad, 0, blocks // 2)
    grad_tokens, first_half = col_reduce_scatter(
        lax.dot_general(
            full_grad, weight, (((1,), (1,)), ((), ())), preferred_element_type=jnp.float32
        ),
        first_half,
    )
    grad_tokens = grad_tokens.astype(jnp.bfloat16)
    if blocks // 2:
        grad_weight = outer_product_sum(local_xt, full_grad, blocks // 2, into=first_half)
    else:
        grad_weight = outer_product_sum(local_xt, full_grad)
    grad_bias = jnp.sum(full_grad.astype(jnp.float32), axis=0)
    return (hidden, grad_tokens, grad_weight, grad_bias)


def solution(mesh):
    placed = (P("col", "row"), P("row", "col"), P("col"), P(None, "col"))
    return jax.shard_map(
        body,
        mesh=mesh,
        in_specs=placed,
        out_specs=(P("row", "col"), P("col", "row"), P("row", "col"), P("col")),
        check_vma=False,
    )
```

```python
import math

import jax
import jax.numpy as jnp
from jax import lax
from jax.experimental import pallas as pl
from jax.experimental.pallas import tpu as pltpu
from jax.sharding import PartitionSpec as P


def activate(preact, cotangent):
    normal_cdf = 0.5 * (1.0 + jax.scipy.special.erf(preact / math.sqrt(2.0)))
    normal_pdf = jnp.exp(-0.5 * preact * preact) / math.sqrt(2.0 * math.pi)
    hidden = (preact * normal_cdf).astype(jnp.bfloat16)
    grad_pre = (cotangent.astype(jnp.float32) * (normal_cdf + preact * normal_pdf)).astype(
        jnp.bfloat16
    )
    return (hidden, grad_pre)


def _outer_kernel(xt_ref, g_ref, o_ref):
    o_ref[...] = jnp.dot(xt_ref[...], g_ref[...], preferred_element_type=jnp.float32).astype(
        o_ref.dtype
    )


def _outer_into_kernel(xt_ref, g_ref, _, o_ref):
    _outer_kernel(xt_ref, g_ref, o_ref)


def outer_product_sum(xt, g, first=0, count=None, into=None, block_m=768, block_n=3072):
    m, k = xt.shape
    n = g.shape[1]
    block_m = min(block_m, m)
    block_n = min(block_n, n)
    if count is None:
        count = m // block_m - first
    in_specs = [
        pl.BlockSpec((block_m, k), lambda j, i: (i + first, 0)),
        pl.BlockSpec((k, block_n), lambda j, i: (0, j)),
    ]
    operands = [xt, g]
    kernel, aliases = _outer_kernel, {}
    if into is not None:
        in_specs.append(pl.BlockSpec(memory_space=pl.ANY))
        operands.append(into)
        kernel, aliases = _outer_into_kernel, {2: 0}
    rows = count * block_m
    return pl.pallas_call(
        kernel,
        grid=(n // block_n, count),
        in_specs=in_specs,
        out_specs=pl.BlockSpec((block_m, block_n), lambda j, i: (i + first, j)),
        out_shape=jax.ShapeDtypeStruct((m, n), jnp.bfloat16),
        input_output_aliases=aliases,
        cost_estimate=pl.CostEstimate(
            flops=2 * rows * n * k, transcendentals=0, bytes_accessed=2 * (rows * k + k * n + rows * n)
        ),
    )(*operands)


def _swap(value, axis, flip):
    size = lax.axis_size(axis)
    return lax.ppermute(value, axis, [(i, i ^ flip) for i in range(size)])


def _pick(index, blocks):
    return lax.dynamic_index_in_dim(blocks, index, axis=0, keepdims=False)


def _halves(value):
    cols = value.shape[1]
    if cols % 256:
        return [value]
    return [value[:, : cols // 2], value[:, cols // 2 :]]


def _bit_orders(n):
    order = list(range(n.bit_length() - 1))
    return [order, order[::-1]]


def row_reduce_scatter(partial, axis="row"):
    n = lax.axis_size(axis)
    if n & (n - 1):
        return lax.psum_scatter(partial, axis, scatter_dimension=0, tiled=True)
    levels = n.bit_length() - 1
    r = lax.axis_index(axis)
    m = partial.shape[0] // n
    outs = []
    for half, order in zip(_halves(partial), _bit_orders(n)):
        cur = half.reshape([2] * levels + [m, half.shape[1]])
        bits = list(range(levels))[::-1]
        for bit in order:
            mine = (r >> bit) & 1
            t = jnp.moveaxis(cur, bits.index(bit), 0)
            sent = _swap(_pick(1 - mine, t).astype(jnp.bfloat16), axis, 1 << bit)
            cur = _pick(mine, t) + sent.astype(jnp.float32)
            bits.remove(bit)
        outs.append(cur.reshape(m, half.shape[1]))
    return jnp.concatenate(outs, axis=1)


def _pair(mine, theirs, bit):
    first = jnp.where(bit == 0, mine, theirs)
    second = jnp.where(bit == 0, theirs, mine)
    return jnp.stack([first, second], axis=0)


def row_all_gather(block, axis="row", order=None):
    n = lax.axis_size(axis)
    if n & (n - 1):
        return lax.all_gather(block, axis, axis=0, tiled=True)
    levels = n.bit_length() - 1
    r = lax.axis_index(axis)
    m = block.shape[0]
    outs = []
    pieces = [(block, order)] if order is not None else zip(_halves(block), _bit_orders(n))
    for half, order in pieces:
        cur = half
        bits = []
        for bit in order:
            cur = _pair(cur, _swap(cur, axis, 1 << bit), (r >> bit) & 1)
            bits.insert(0, bit)
        perm = sorted(range(levels), key=lambda j: -bits[j])
        cur = jnp.transpose(cur, perm + [levels, levels + 1])
        outs.append(cur.reshape(n * m, half.shape[1]))
    return jnp.concatenate(outs, axis=1)


def col_all_gather(block, axis="col"):
    n = lax.axis_size(axis)
    if n % 2:
        return lax.all_gather(block, axis, axis=0, tiled=True)
    groups = [list(range(k, n, 2)) for k in range(2)]
    mine = lax.all_gather(block, axis, axis_index_groups=groups)
    both = _pair(mine, _swap(mine, axis, 1), lax.axis_index(axis) % 2)
    return jnp.swapaxes(both, 0, 1).reshape(n * block.shape[0], block.shape[1])


def col_reduce_scatter(partial, hold, axis="col"):
    n = lax.axis_size(axis)
    if n % 2:
        return lax.psum_scatter(partial, axis, scatter_dimension=0, tiled=True), hold
    m = partial.shape[0] // n
    k = lax.axis_index(axis) % 2
    by_core = jnp.swapaxes(partial.reshape(n // 2, 2, m, partial.shape[1]), 0, 1)
    moved = _swap(_pick(1 - k, by_core).astype(jnp.bfloat16), axis, 1)
    chip = _pick(k, by_core) + moved.astype(jnp.float32)
    chips = n // 2
    z = lax.axis_index(axis) // 2
    if chips & (chips - 1):
        total = _pick(z, chip)
        for d in range(1, chips):
            pairs = [(2 * i + j, 2 * ((i + d) % chips) + j) for i in range(chips) for j in range(2)]
            total = total + lax.ppermute(_pick((z + d) % chips, chip), axis, pairs)
        return total, hold
    levels = chips.bit_length() - 1
    cur = chip.reshape([2] * levels + [m, partial.shape[1]])
    bits = list(range(levels))[::-1]
    for bit in range(levels):
        mine = (z >> bit) & 1
        t = jnp.moveaxis(cur, bits.index(bit), 0)
        sent = _swap(_pick(1 - mine, t).astype(jnp.bfloat16), axis, 2 << bit)
        cur = _pick(mine, t) + sent.astype(jnp.float32)
        bits.remove(bit)
        if bit == 0:
            cur, hold = lax.optimization_barrier((cur, hold))
    return cur.reshape(m, partial.shape[1]), hold


def body(tokens, weight, bias, cotangent):
    local_x = col_all_gather(tokens)
    my_rows = local_x.shape[0] // lax.axis_size("row")
    first_row = lax.axis_index("row") * my_rows
    partial_value = jnp.dot(local_x, weight, preferred_element_type=jnp.float32)
    my_cot = lax.dynamic_slice_in_dim(cotangent, first_row, my_rows, 0)
    preact = row_reduce_scatter(partial_value)
    hidden, full_grad, start = [], [], 0
    orders = _bit_orders(lax.axis_size("row"))
    for number, part in enumerate(_halves(preact)):
        cols = slice(start, start + part.shape[1])
        h, g = activate(part + bias[cols], my_cot[:, cols])
        hidden.append(h)
        full_grad.append(row_all_gather(g, order=orders[number % 2]))
        start += part.shape[1]
    hidden = jnp.concatenate(hidden, axis=1)
    full_grad = jnp.concatenate(full_grad, axis=1)
    local_xt = local_x.T
    blocks = local_xt.shape[0] // min(768, local_xt.shape[0])
    first_half = outer_product_sum(local_xt, full_grad, 0, blocks // 2)
    grad_tokens, first_half = col_reduce_scatter(
        lax.dot_general(
            full_grad, weight, (((1,), (1,)), ((), ())), preferred_element_type=jnp.float32
        ),
        first_half,
    )
    grad_tokens = grad_tokens.astype(jnp.bfloat16)
    if blocks // 2:
        grad_weight = outer_product_sum(local_xt, full_grad, blocks // 2, into=first_half)
    else:
        grad_weight = outer_product_sum(local_xt, full_grad)
    grad_bias = jnp.sum(full_grad.astype(jnp.float32), axis=0)
    return (hidden, grad_tokens, grad_weight, grad_bias)


def solution(mesh):
    placed = (P("col", "row"), P("row", "col"), P("col"), P(None, "col"))
    return jax.shard_map(
        body,
        mesh=mesh,
        in_specs=placed,
        out_specs=(P("row", "col"), P("col", "row"), P("row", "col"), P("col")),
        check_vma=False,
    )
```

```python
import math

import jax
import jax.numpy as jnp
from jax import lax
from jax.experimental import pallas as pl
from jax.experimental.pallas import tpu as pltpu
from jax.sharding import PartitionSpec as P


def activate(preact, cotangent):
    normal_cdf = 0.5 * (1.0 + jax.scipy.special.erf(preact / math.sqrt(2.0)))
    normal_pdf = jnp.exp(-0.5 * preact * preact) / math.sqrt(2.0 * math.pi)
    hidden = (preact * normal_cdf).astype(jnp.bfloat16)
    grad_pre = (cotangent.astype(jnp.float32) * (normal_cdf + preact * normal_pdf)).astype(
        jnp.bfloat16
    )
    return (hidden, grad_pre)


def _outer_kernel(xt_ref, g_ref, o_ref):
    o_ref[...] = jnp.dot(xt_ref[...], g_ref[...], preferred_element_type=jnp.float32).astype(
        o_ref.dtype
    )


def _outer_into_kernel(xt_ref, g_ref, _, o_ref):
    _outer_kernel(xt_ref, g_ref, o_ref)


def outer_product_sum(xt, g, first=0, count=None, into=None, block_m=768, block_n=3072):
    m, k = xt.shape
    n = g.shape[1]
    block_m = min(block_m, m)
    block_n = min(block_n, n)
    if count is None:
        count = m // block_m - first
    in_specs = [
        pl.BlockSpec((block_m, k), lambda j, i: (i + first, 0)),
        pl.BlockSpec((k, block_n), lambda j, i: (0, j)),
    ]
    operands = [xt, g]
    kernel, aliases = _outer_kernel, {}
    if into is not None:
        in_specs.append(pl.BlockSpec(memory_space=pl.ANY))
        operands.append(into)
        kernel, aliases = _outer_into_kernel, {2: 0}
    rows = count * block_m
    return pl.pallas_call(
        kernel,
        grid=(n // block_n, count),
        in_specs=in_specs,
        out_specs=pl.BlockSpec((block_m, block_n), lambda j, i: (i + first, j)),
        out_shape=jax.ShapeDtypeStruct((m, n), jnp.bfloat16),
        input_output_aliases=aliases,
        cost_estimate=pl.CostEstimate(
            flops=2 * rows * n * k, transcendentals=0, bytes_accessed=2 * (rows * k + k * n + rows * n)
        ),
    )(*operands)


def _swap(value, axis, flip):
    size = lax.axis_size(axis)
    return lax.ppermute(value, axis, [(i, i ^ flip) for i in range(size)])


def _pick(index, blocks):
    return lax.dynamic_index_in_dim(blocks, index, axis=0, keepdims=False)


def _halves(value):
    cols = value.shape[1]
    if cols % 256:
        return [value]
    return [value[:, : cols // 2], value[:, cols // 2 :]]


def _bit_orders(n):
    order = list(range(n.bit_length() - 1))
    return [order, order[::-1]]


def row_reduce_scatter(partial, axis="row"):
    n = lax.axis_size(axis)
    if n & (n - 1):
        return lax.psum_scatter(partial, axis, scatter_dimension=0, tiled=True)
    levels = n.bit_length() - 1
    r = lax.axis_index(axis)
    m = partial.shape[0] // n
    outs = []
    for half, order in zip(_halves(partial), _bit_orders(n)):
        cur = half.reshape([2] * levels + [m, half.shape[1]])
        bits = list(range(levels))[::-1]
        for bit in order:
            mine = (r >> bit) & 1
            t = jnp.moveaxis(cur, bits.index(bit), 0)
            sent = _swap(_pick(1 - mine, t).astype(jnp.bfloat16), axis, 1 << bit)
            cur = _pick(mine, t) + sent.astype(jnp.float32)
            bits.remove(bit)
        outs.append(cur.reshape(m, half.shape[1]))
    return jnp.concatenate(outs, axis=1)


def _pair(mine, theirs, bit):
    first = jnp.where(bit == 0, mine, theirs)
    second = jnp.where(bit == 0, theirs, mine)
    return jnp.stack([first, second], axis=0)


def row_all_gather(block, axis="row", order=None):
    n = lax.axis_size(axis)
    if n & (n - 1):
        return lax.all_gather(block, axis, axis=0, tiled=True)
    levels = n.bit_length() - 1
    r = lax.axis_index(axis)
    m = block.shape[0]
    outs = []
    pieces = [(block, order)] if order is not None else zip(_halves(block), _bit_orders(n))
    for half, order in pieces:
        cur = half
        bits = []
        for bit in order:
            cur = _pair(cur, _swap(cur, axis, 1 << bit), (r >> bit) & 1)
            bits.insert(0, bit)
        perm = sorted(range(levels), key=lambda j: -bits[j])
        cur = jnp.transpose(cur, perm + [levels, levels + 1])
        outs.append(cur.reshape(n * m, half.shape[1]))
    return jnp.concatenate(outs, axis=1)


def col_all_gather(block, axis="col"):
    n = lax.axis_size(axis)
    if n % 2:
        return lax.all_gather(block, axis, axis=0, tiled=True)
    groups = [list(range(k, n, 2)) for k in range(2)]
    mine = lax.all_gather(block, axis, axis_index_groups=groups)
    both = _pair(mine, _swap(mine, axis, 1), lax.axis_index(axis) % 2)
    return jnp.swapaxes(both, 0, 1).reshape(n * block.shape[0], block.shape[1])


def col_reduce_scatter(partial, hold, axis="col"):
    n = lax.axis_size(axis)
    if n % 2:
        return lax.psum_scatter(partial, axis, scatter_dimension=0, tiled=True), hold
    m = partial.shape[0] // n
    k = lax.axis_index(axis) % 2
    by_core = jnp.swapaxes(partial.reshape(n // 2, 2, m, partial.shape[1]), 0, 1)
    moved = _swap(_pick(1 - k, by_core).astype(jnp.bfloat16), axis, 1)
    chip = _pick(k, by_core) + moved.astype(jnp.float32)
    chips = n // 2
    z = lax.axis_index(axis) // 2
    if chips & (chips - 1):
        total = _pick(z, chip)
        for d in range(1, chips):
            pairs = [(2 * i + j, 2 * ((i + d) % chips) + j) for i in range(chips) for j in range(2)]
            total = total + lax.ppermute(_pick((z + d) % chips, chip), axis, pairs)
        return total, hold
    levels = chips.bit_length() - 1
    cur = chip.reshape([2] * levels + [m, partial.shape[1]])
    bits = list(range(levels))[::-1]
    for bit in range(levels):
        mine = (z >> bit) & 1
        t = jnp.moveaxis(cur, bits.index(bit), 0)
        sent = _swap(_pick(1 - mine, t).astype(jnp.bfloat16), axis, 2 << bit)
        cur = _pick(mine, t) + sent.astype(jnp.float32)
        bits.remove(bit)
        if bit == 0:
            cur, hold = lax.optimization_barrier((cur, hold))
    return cur.reshape(m, partial.shape[1]), hold


def _grad_tokens_partial(grad_parts, weight):
    total, start = None, 0
    for part in grad_parts:
        cols = slice(start, start + part.shape[1])
        term = lax.dot_general(
            part, weight[:, cols], (((1,), (1,)), ((), ())), preferred_element_type=jnp.float32
        )
        total = term if total is None else total + term
        start += part.shape[1]
    return total


def body(tokens, weight, bias, cotangent):
    local_x = col_all_gather(tokens)
    my_rows = local_x.shape[0] // lax.axis_size("row")
    first_row = lax.axis_index("row") * my_rows
    partial_value = jnp.dot(local_x, weight, preferred_element_type=jnp.float32)
    my_cot = lax.dynamic_slice_in_dim(cotangent, first_row, my_rows, 0)
    preact = row_reduce_scatter(partial_value)
    hidden, full_grad, start = [], [], 0
    orders = _bit_orders(lax.axis_size("row"))
    for number, part in enumerate(_halves(preact)):
        cols = slice(start, start + part.shape[1])
        h, g = activate(part + bias[cols], my_cot[:, cols])
        hidden.append(h)
        full_grad.append(row_all_gather(g, order=orders[number % 2]))
        start += part.shape[1]
    hidden = jnp.concatenate(hidden, axis=1)
    grad_parts = full_grad
    full_grad = jnp.concatenate(grad_parts, axis=1)
    local_xt = local_x.T
    blocks = local_xt.shape[0] // min(768, local_xt.shape[0])
    first_half = outer_product_sum(local_xt, full_grad, 0, blocks // 2)
    grad_tokens, first_half = col_reduce_scatter(
        _grad_tokens_partial(grad_parts, weight),
        first_half,
    )
    grad_tokens = grad_tokens.astype(jnp.bfloat16)
    if blocks // 2:
        grad_weight = outer_product_sum(local_xt, full_grad, blocks // 2, into=first_half)
    else:
        grad_weight = outer_product_sum(local_xt, full_grad)
    grad_bias = jnp.sum(full_grad.astype(jnp.float32), axis=0)
    return (hidden, grad_tokens, grad_weight, grad_bias)


def solution(mesh):
    placed = (P("col", "row"), P("row", "col"), P("col"), P(None, "col"))
    return jax.shard_map(
        body,
        mesh=mesh,
        in_specs=placed,
        out_specs=(P("row", "col"), P("col", "row"), P("row", "col"), P("col")),
        check_vma=False,
    )
```

```python
import math

import jax
import jax.numpy as jnp
from jax import lax
from jax.experimental import pallas as pl
from jax.experimental.pallas import tpu as pltpu
from jax.sharding import PartitionSpec as P


def activate(preact, cotangent):
    normal_cdf = 0.5 * (1.0 + jax.scipy.special.erf(preact / math.sqrt(2.0)))
    normal_pdf = jnp.exp(-0.5 * preact * preact) / math.sqrt(2.0 * math.pi)
    hidden = (preact * normal_cdf).astype(jnp.bfloat16)
    grad_pre = (cotangent.astype(jnp.float32) * (normal_cdf + preact * normal_pdf)).astype(
        jnp.bfloat16
    )
    return (hidden, grad_pre)


def _outer_kernel(xt_ref, g_ref, o_ref):
    o_ref[...] = jnp.dot(xt_ref[...], g_ref[...], preferred_element_type=jnp.float32).astype(
        o_ref.dtype
    )


def _outer_into_kernel(xt_ref, g_ref, _, o_ref):
    _outer_kernel(xt_ref, g_ref, o_ref)


def outer_product_sum(xt, g, first=0, count=None, into=None, block_m=768, block_n=3072):
    m, k = xt.shape
    n = g.shape[1]
    block_m = min(block_m, m)
    block_n = min(block_n, n)
    if count is None:
        count = m // block_m - first
    in_specs = [
        pl.BlockSpec((block_m, k), lambda j, i: (i + first, 0)),
        pl.BlockSpec((k, block_n), lambda j, i: (0, j)),
    ]
    operands = [xt, g]
    kernel, aliases = _outer_kernel, {}
    if into is not None:
        in_specs.append(pl.BlockSpec(memory_space=pl.ANY))
        operands.append(into)
        kernel, aliases = _outer_into_kernel, {2: 0}
    rows = count * block_m
    return pl.pallas_call(
        kernel,
        grid=(n // block_n, count),
        in_specs=in_specs,
        out_specs=pl.BlockSpec((block_m, block_n), lambda j, i: (i + first, j)),
        out_shape=jax.ShapeDtypeStruct((m, n), jnp.bfloat16),
        input_output_aliases=aliases,
        cost_estimate=pl.CostEstimate(
            flops=2 * rows * n * k, transcendentals=0, bytes_accessed=2 * (rows * k + k * n + rows * n)
        ),
    )(*operands)


def _swap(value, axis, flip):
    size = lax.axis_size(axis)
    return lax.ppermute(value, axis, [(i, i ^ flip) for i in range(size)])


def _pick(index, blocks):
    return lax.dynamic_index_in_dim(blocks, index, axis=0, keepdims=False)


def _halves(value):
    cols = value.shape[1]
    if cols % 256:
        return [value]
    return [value[:, : cols // 2], value[:, cols // 2 :]]


def _bit_orders(n):
    order = list(range(n.bit_length() - 1))
    return [order, order[::-1]]


def row_reduce_scatter(partial, axis="row"):
    n = lax.axis_size(axis)
    if n & (n - 1):
        return lax.psum_scatter(partial, axis, scatter_dimension=0, tiled=True)
    levels = n.bit_length() - 1
    r = lax.axis_index(axis)
    m = partial.shape[0] // n
    outs = []
    for half, order in zip(_halves(partial), _bit_orders(n)):
        cur = half.reshape([2] * levels + [m, half.shape[1]])
        bits = list(range(levels))[::-1]
        for bit in order:
            mine = (r >> bit) & 1
            t = jnp.moveaxis(cur, bits.index(bit), 0)
            sent = _swap(_pick(1 - mine, t).astype(jnp.bfloat16), axis, 1 << bit)
            cur = _pick(mine, t) + sent.astype(jnp.float32)
            bits.remove(bit)
        outs.append(cur.reshape(m, half.shape[1]))
    return jnp.concatenate(outs, axis=1)


def _pair(mine, theirs, bit):
    first = jnp.where(bit == 0, mine, theirs)
    second = jnp.where(bit == 0, theirs, mine)
    return jnp.stack([first, second], axis=0)


def row_all_gather(block, axis="row", order=None):
    n = lax.axis_size(axis)
    if n & (n - 1):
        return lax.all_gather(block, axis, axis=0, tiled=True)
    levels = n.bit_length() - 1
    r = lax.axis_index(axis)
    m = block.shape[0]
    outs = []
    pieces = [(block, order)] if order is not None else zip(_halves(block), _bit_orders(n))
    for half, order in pieces:
        cur = half
        bits = []
        for bit in order:
            cur = _pair(cur, _swap(cur, axis, 1 << bit), (r >> bit) & 1)
            bits.insert(0, bit)
        perm = sorted(range(levels), key=lambda j: -bits[j])
        cur = jnp.transpose(cur, perm + [levels, levels + 1])
        outs.append(cur.reshape(n * m, half.shape[1]))
    return jnp.concatenate(outs, axis=1)


def col_all_gather(block, axis="col"):
    n = lax.axis_size(axis)
    if n % 2:
        return lax.all_gather(block, axis, axis=0, tiled=True)
    chips = n // 2
    c = lax.axis_index(axis)
    z, k = c // 2, c % 2
    held = [block]
    for d in range(1, chips):
        for step in (d, -d):
            pairs = [
                (2 * i + j, 2 * (i + step) + j)
                for i in range(chips)
                if 0 <= i + step < chips
                for j in range(2)
            ]
            held.append(lax.ppermute(block, axis, pairs))
    held = jnp.stack(held)
    mine = []
    for j in range(chips):
        at = jnp.where(j == z, 0, jnp.where(j < z, 2 * (z - j) - 1, 2 * (j - z)))
        mine.append(_pick(at, held))
    mine = jnp.stack(mine)
    both = _pair(mine, _swap(mine, axis, 1), k)
    return jnp.swapaxes(both, 0, 1).reshape(n * block.shape[0], block.shape[1])


def col_reduce_scatter(partial, hold, axis="col"):
    n = lax.axis_size(axis)
    if n % 2:
        return lax.psum_scatter(partial, axis, scatter_dimension=0, tiled=True), hold
    m = partial.shape[0] // n
    k = lax.axis_index(axis) % 2
    by_core = jnp.swapaxes(partial.reshape(n // 2, 2, m, partial.shape[1]), 0, 1)
    moved = _swap(_pick(1 - k, by_core).astype(jnp.bfloat16), axis, 1)
    chip = _pick(k, by_core) + moved.astype(jnp.float32)
    chips = n // 2
    z = lax.axis_index(axis) // 2
    if chips & (chips - 1):
        total = _pick(z, chip)
        for d in range(1, chips):
            pairs = [(2 * i + j, 2 * ((i + d) % chips) + j) for i in range(chips) for j in range(2)]
            total = total + lax.ppermute(_pick((z + d) % chips, chip), axis, pairs)
        return total, hold
    levels = chips.bit_length() - 1
    cur = chip.reshape([2] * levels + [m, partial.shape[1]])
    bits = list(range(levels))[::-1]
    for bit in range(levels):
        mine = (z >> bit) & 1
        t = jnp.moveaxis(cur, bits.index(bit), 0)
        sent = _swap(_pick(1 - mine, t).astype(jnp.bfloat16), axis, 2 << bit)
        cur = _pick(mine, t) + sent.astype(jnp.float32)
        bits.remove(bit)
        if bit == 0:
            cur, hold = lax.optimization_barrier((cur, hold))
    return cur.reshape(m, partial.shape[1]), hold


def body(tokens, weight, bias, cotangent):
    local_x = col_all_gather(tokens)
    my_rows = local_x.shape[0] // lax.axis_size("row")
    first_row = lax.axis_index("row") * my_rows
    partial_value = jnp.dot(local_x, weight, preferred_element_type=jnp.float32)
    my_cot = lax.dynamic_slice_in_dim(cotangent, first_row, my_rows, 0)
    preact = row_reduce_scatter(partial_value)
    hidden, full_grad, start = [], [], 0
    orders = _bit_orders(lax.axis_size("row"))
    for number, part in enumerate(_halves(preact)):
        cols = slice(start, start + part.shape[1])
        h, g = activate(part + bias[cols], my_cot[:, cols])
        hidden.append(h)
        full_grad.append(row_all_gather(g, order=orders[number % 2]))
        start += part.shape[1]
    hidden = jnp.concatenate(hidden, axis=1)
    full_grad = jnp.concatenate(full_grad, axis=1)
    local_xt = local_x.T
    blocks = local_xt.shape[0] // min(768, local_xt.shape[0])
    first_half = outer_product_sum(local_xt, full_grad, 0, blocks // 2)
    grad_tokens, first_half = col_reduce_scatter(
        lax.dot_general(
            full_grad, weight, (((1,), (1,)), ((), ())), preferred_element_type=jnp.float32
        ),
        first_half,
    )
    grad_tokens = grad_tokens.astype(jnp.bfloat16)
    if blocks // 2:
        grad_weight = outer_product_sum(local_xt, full_grad, blocks // 2, into=first_half)
    else:
        grad_weight = outer_product_sum(local_xt, full_grad)
    grad_bias = jnp.sum(full_grad.astype(jnp.float32), axis=0)
    return (hidden, grad_tokens, grad_weight, grad_bias)


def solution(mesh):
    placed = (P("col", "row"), P("row", "col"), P("col"), P(None, "col"))
    return jax.shard_map(
        body,
        mesh=mesh,
        in_specs=placed,
        out_specs=(P("row", "col"), P("col", "row"), P("row", "col"), P("col")),
        check_vma=False,
    )
```

```python
import math

import jax
import jax.numpy as jnp
from jax import lax
from jax.experimental import pallas as pl
from jax.experimental.pallas import tpu as pltpu
from jax.sharding import PartitionSpec as P


def activate(preact, cotangent):
    normal_cdf = 0.5 * (1.0 + jax.scipy.special.erf(preact / math.sqrt(2.0)))
    normal_pdf = jnp.exp(-0.5 * preact * preact) / math.sqrt(2.0 * math.pi)
    hidden = (preact * normal_cdf).astype(jnp.bfloat16)
    grad_pre = (cotangent.astype(jnp.float32) * (normal_cdf + preact * normal_pdf)).astype(
        jnp.bfloat16
    )
    return (hidden, grad_pre)


def _outer_kernel(xt_ref, g_ref, o_ref):
    o_ref[...] = jnp.dot(xt_ref[...], g_ref[...], preferred_element_type=jnp.float32).astype(
        o_ref.dtype
    )


def _outer_into_kernel(xt_ref, g_ref, _, o_ref):
    _outer_kernel(xt_ref, g_ref, o_ref)


def outer_product_sum(xt, g, first=0, count=None, into=None, block_m=768, block_n=3072):
    m, k = xt.shape
    n = g.shape[1]
    block_m = min(block_m, m)
    block_n = min(block_n, n)
    if count is None:
        count = m // block_m - first
    in_specs = [
        pl.BlockSpec((block_m, k), lambda j, i: (i + first, 0)),
        pl.BlockSpec((k, block_n), lambda j, i: (0, j)),
    ]
    operands = [xt, g]
    kernel, aliases = _outer_kernel, {}
    if into is not None:
        in_specs.append(pl.BlockSpec(memory_space=pl.ANY))
        operands.append(into)
        kernel, aliases = _outer_into_kernel, {2: 0}
    rows = count * block_m
    return pl.pallas_call(
        kernel,
        grid=(n // block_n, count),
        in_specs=in_specs,
        out_specs=pl.BlockSpec((block_m, block_n), lambda j, i: (i + first, j)),
        out_shape=jax.ShapeDtypeStruct((m, n), jnp.bfloat16),
        input_output_aliases=aliases,
        cost_estimate=pl.CostEstimate(
            flops=2 * rows * n * k, transcendentals=0, bytes_accessed=2 * (rows * k + k * n + rows * n)
        ),
    )(*operands)


def _swap(value, axis, flip):
    size = lax.axis_size(axis)
    return lax.ppermute(value, axis, [(i, i ^ flip) for i in range(size)])


def _pick(index, blocks):
    return lax.dynamic_index_in_dim(blocks, index, axis=0, keepdims=False)


def _halves(value):
    cols = value.shape[1]
    if cols % 256:
        return [value]
    return [value[:, : cols // 2], value[:, cols // 2 :]]


def _bit_orders(n):
    order = list(range(n.bit_length() - 1))
    return [order, order[::-1]]


def row_reduce_scatter(partial, axis="row", order=None):
    n = lax.axis_size(axis)
    if n & (n - 1):
        return lax.psum_scatter(partial, axis, scatter_dimension=0, tiled=True)
    levels = n.bit_length() - 1
    r = lax.axis_index(axis)
    m = partial.shape[0] // n
    outs = []
    pieces = [(partial, order)] if order is not None else zip(_halves(partial), _bit_orders(n))
    for half, order in pieces:
        cur = half.reshape([2] * levels + [m, half.shape[1]])
        bits = list(range(levels))[::-1]
        for bit in order:
            mine = (r >> bit) & 1
            t = jnp.moveaxis(cur, bits.index(bit), 0)
            sent = _swap(_pick(1 - mine, t).astype(jnp.bfloat16), axis, 1 << bit)
            cur = _pick(mine, t) + sent.astype(jnp.float32)
            bits.remove(bit)
        outs.append(cur.reshape(m, half.shape[1]))
    return jnp.concatenate(outs, axis=1)


def _pair(mine, theirs, bit):
    first = jnp.where(bit == 0, mine, theirs)
    second = jnp.where(bit == 0, theirs, mine)
    return jnp.stack([first, second], axis=0)


def row_all_gather(block, axis="row", order=None):
    n = lax.axis_size(axis)
    if n & (n - 1):
        return lax.all_gather(block, axis, axis=0, tiled=True)
    levels = n.bit_length() - 1
    r = lax.axis_index(axis)
    m = block.shape[0]
    outs = []
    pieces = [(block, order)] if order is not None else zip(_halves(block), _bit_orders(n))
    for half, order in pieces:
        cur = half
        bits = []
        for bit in order:
            cur = _pair(cur, _swap(cur, axis, 1 << bit), (r >> bit) & 1)
            bits.insert(0, bit)
        perm = sorted(range(levels), key=lambda j: -bits[j])
        cur = jnp.transpose(cur, perm + [levels, levels + 1])
        outs.append(cur.reshape(n * m, half.shape[1]))
    return jnp.concatenate(outs, axis=1)


def col_all_gather(block, axis="col"):
    n = lax.axis_size(axis)
    if n % 2:
        return lax.all_gather(block, axis, axis=0, tiled=True)
    groups = [list(range(k, n, 2)) for k in range(2)]
    mine = lax.all_gather(block, axis, axis_index_groups=groups)
    both = _pair(mine, _swap(mine, axis, 1), lax.axis_index(axis) % 2)
    return jnp.swapaxes(both, 0, 1).reshape(n * block.shape[0], block.shape[1])


def col_reduce_scatter(partial, hold, axis="col"):
    n = lax.axis_size(axis)
    if n % 2:
        return lax.psum_scatter(partial, axis, scatter_dimension=0, tiled=True), hold
    m = partial.shape[0] // n
    k = lax.axis_index(axis) % 2
    by_core = jnp.swapaxes(partial.reshape(n // 2, 2, m, partial.shape[1]), 0, 1)
    moved = _swap(_pick(1 - k, by_core).astype(jnp.bfloat16), axis, 1)
    chip = _pick(k, by_core) + moved.astype(jnp.float32)
    chips = n // 2
    z = lax.axis_index(axis) // 2
    if chips & (chips - 1):
        total = _pick(z, chip)
        for d in range(1, chips):
            pairs = [(2 * i + j, 2 * ((i + d) % chips) + j) for i in range(chips) for j in range(2)]
            total = total + lax.ppermute(_pick((z + d) % chips, chip), axis, pairs)
        return total, hold
    levels = chips.bit_length() - 1
    cur = chip.reshape([2] * levels + [m, partial.shape[1]])
    bits = list(range(levels))[::-1]
    for bit in range(levels):
        mine = (z >> bit) & 1
        t = jnp.moveaxis(cur, bits.index(bit), 0)
        sent = _swap(_pick(1 - mine, t).astype(jnp.bfloat16), axis, 2 << bit)
        cur = _pick(mine, t) + sent.astype(jnp.float32)
        bits.remove(bit)
        if bit == 0:
            cur, hold = lax.optimization_barrier((cur, hold))
    return cur.reshape(m, partial.shape[1]), hold


def body(tokens, weight, bias, cotangent):
    local_x = col_all_gather(tokens)
    my_rows = local_x.shape[0] // lax.axis_size("row")
    first_row = lax.axis_index("row") * my_rows
    width = weight.shape[1]
    split = width // 2 if width % 256 == 0 else width
    my_cot = lax.dynamic_slice_in_dim(cotangent, first_row, my_rows, 0)
    hidden, full_grad, start = [], [], 0
    orders = _bit_orders(lax.axis_size("row"))
    row_size = lax.axis_size("row")
    for number, lo in enumerate(range(0, width, split)):
        part = jnp.dot(local_x, weight[:, lo : lo + split], preferred_element_type=jnp.float32)
        if row_size & (row_size - 1):
            part = row_reduce_scatter(part)
        else:
            part = row_reduce_scatter(part, order=orders[number % 2])
        cols = slice(start, start + part.shape[1])
        h, g = activate(part + bias[cols], my_cot[:, cols])
        hidden.append(h)
        full_grad.append(row_all_gather(g, order=orders[number % 2]))
        start += part.shape[1]
    hidden = jnp.concatenate(hidden, axis=1)
    full_grad = jnp.concatenate(full_grad, axis=1)
    local_xt = local_x.T
    blocks = local_xt.shape[0] // min(768, local_xt.shape[0])
    first_half = outer_product_sum(local_xt, full_grad, 0, blocks // 2)
    grad_tokens, first_half = col_reduce_scatter(
        lax.dot_general(
            full_grad, weight, (((1,), (1,)), ((), ())), preferred_element_type=jnp.float32
        ),
        first_half,
    )
    grad_tokens = grad_tokens.astype(jnp.bfloat16)
    if blocks // 2:
        grad_weight = outer_product_sum(local_xt, full_grad, blocks // 2, into=first_half)
    else:
        grad_weight = outer_product_sum(local_xt, full_grad)
    grad_bias = jnp.sum(full_grad.astype(jnp.float32), axis=0)
    return (hidden, grad_tokens, grad_weight, grad_bias)


def solution(mesh):
    placed = (P("col", "row"), P("row", "col"), P("col"), P(None, "col"))
    return jax.shard_map(
        body,
        mesh=mesh,
        in_specs=placed,
        out_specs=(P("row", "col"), P("col", "row"), P("row", "col"), P("col")),
        check_vma=False,
    )
```
